1024 devices in a mesh: grp: 16 (over y, z_hi), dev: 64 (over z_lo, x, core).
Axes of the slice: x: 4, y: 4, z: 32 (z_hi: 4, z_lo: 8; z = z_hi * 8 + z_lo), core: 2. Of those that a mesh axis runs over, the one named last changes fastest.
Arguments:
- amplitudes: float32 [2, 16, 64, 8192], P(None, 'grp', 'dev'), may hold values from -6 to 6
- joined_gates: float32 [4, 2, 128, 128], replicated, may hold values from -0.375 to 0.375
- pair_gate: float32 [2, 4, 4], replicated, may hold values from -2 to 2
- layout_in: int32 [23], replicated, may hold values from 0 to 22, as said below
- layout_out: int32 [23], replicated, may hold values from 0 to 22, as said below
- gate_qubits: int32 [4, 7], replicated, may hold values from 0 to 22, as said below
- spare_values: int32 [10], replicated, may hold values from 0 to 1
Outputs:
- evolved: float32 [2, 16, 64, 8192], P(None, 'grp', 'dev')
The draws below stay inside these ranges and needn't reach their ends.
Inputs may be any that keep to these rules, and one draw needn't show every extreme that they name: `layout_in`: a permutation of the qubits. `layout_out`: a permutation of the qubits; entries 13 + 6 onward equal those of layout_in; entries 13 to 18 are qubits that layout_in holds below position 13. `gate_qubits`: each row holds 7 different qubits; rows 0 and 1 name qubits that layout_in holds below position 13, rows 2 and 3 qubits that layout_out holds below position 13.
All inputs are finite; a program needn't handle non-finite values.
Results may differ from the reference program's by a relative error of at most 0.0001.
Values sent between devices are 32-bit elements; how exact they have to be, the bound alone decides.
No kernel may reach another device: no remote copies, remote signals or barrier semaphores. Data moves between devices by JAX's collectives and lax.ppermute only.
A program may use at most 32 MiB of HBM per device.

```python
import jax
import jax.numpy as jnp
from jax import lax

AMPS = 8192
GATES = 4
GATE_QUBITS = 7
SPARE = 10
SPAN = 128
LQ = 13
DQ = 6
GQ = 4
N_GRP = 16
N_DEV = 64


def layouts(key):
    base_key = jax.random.fold_in(key, 4099)
    subkeys = jax.random.split(base_key, 7)
    qubit_count = LQ + DQ + GQ
    layout_in = jax.random.permutation(subkeys[0], qubit_count).astype(jnp.int32)
    local_in = layout_in[:LQ]
    shuffled = jax.random.permutation(subkeys[1], local_in)
    leaving = shuffled[:DQ]
    staying = jnp.concatenate([shuffled[DQ:], layout_in[LQ:LQ + DQ]])
    local_out = jax.random.permutation(subkeys[2], staying)
    layout_out = jnp.concatenate([local_out, leaving, layout_in[LQ + DQ:]]).astype(jnp.int32)
    gate_rows = []
    for gate_num in range(4):
        source_set = local_in if gate_num < 2 else local_out
        gate_rows.append(jax.random.permutation(subkeys[3 + gate_num], source_set)[:GATE_QUBITS])
    return (layout_in, layout_out, jnp.stack(gate_rows).astype(jnp.int32))


def draw_layout_in(key, part):
    return layouts(key)[0]


def draw_layout_out(key, part):
    return layouts(key)[1]


def draw_gate_qubits(key, part):
    return layouts(key)[2]


def plant(values, stream_key, least, high):
    shape = values.shape
    spot = [jax.random.randint(jax.random.fold_in(stream_key, axis), (), 0, shape[axis]) for axis in range(len(shape))]
    values = values.at[tuple(spot)].set(least)
    longest = shape.index(max(shape))
    spot[longest] = (spot[longest] + 1) % shape[longest]
    return values.at[tuple(spot)].set(high)


def block_levels(own_key, dims, cuts, smallest, top_value):
    level = 1.0
    for axis_at, blocks in cuts:
        steps = jax.random.uniform(jax.random.fold_in(jax.random.fold_in(own_key, 6), axis_at), (blocks,), jnp.float32, smallest / len(cuts), top_value / len(cuts))
        level = level * jnp.repeat(jnp.exp(steps), dims[axis_at] // blocks).reshape((-1,) + (1,) * (len(dims) - 1 - axis_at))
    return level


def normal_values(stream_key, dims, scale, reach, cuts=(), kind=jnp.bfloat16):
    array = jax.random.normal(stream_key, dims, jnp.float32) * scale
    if len(cuts) > 0:
        array = block_levels(stream_key, dims, cuts, -0.22, 0.18) * array
    return jnp.clip(array, min=-reach, max=reach).astype(kind)


def setup_inputs(seed: int = 0) -> dict:
    seeds = jax.random.split(jax.random.key(seed), 8)
    amplitudes = normal_values(seeds[0], (2, N_GRP, N_DEV, AMPS), 1.0, 6.0, ((1, 16), (2, 64)), jnp.float32)
    joined_gates = normal_values(seeds[1], (GATES, 2, SPAN, SPAN), (2 * SPAN) ** -0.5, 0.375, (), jnp.float32)
    pair_gate = normal_values(seeds[2], (2, 4, 4), 8 ** -0.5, 2.0, (), jnp.float32)
    layout_in = draw_layout_in(jax.random.fold_in(seeds[7], 71), 0)
    layout_out = draw_layout_out(jax.random.fold_in(seeds[7], 71), 0)
    gate_qubits = draw_gate_qubits(jax.random.fold_in(seeds[7], 71), 0)
    spare_values = plant(jax.random.randint(seeds[6], (SPARE,), 0, 2), jax.random.fold_in(seeds[6], 1), 0, 1).astype(jnp.int32)
    return dict(amplitudes=amplitudes, joined_gates=joined_gates, pair_gate=pair_gate, layout_in=layout_in, layout_out=layout_out, gate_qubits=gate_qubits, spare_values=spare_values)


HIGHEST = lax.Precision.HIGHEST


def source_index(bit_order, bit_count):
    position = jnp.arange(2 ** bit_count, dtype=jnp.int32)
    source = jnp.zeros((2 ** bit_count,), jnp.int32)
    for place_bit in range(bit_count):
        source = source + jnp.left_shift(jnp.right_shift(position, place_bit) & 1, bit_order[place_bit])
    return source


def complex_gate(values, matrix):
    real_part = jnp.dot(values[0], matrix[0].T, precision=HIGHEST, preferred_element_type=jnp.float32) - jnp.dot(values[1], matrix[1].T, precision=HIGHEST, preferred_element_type=jnp.float32)
    imag_part = jnp.dot(values[0], matrix[1].T, precision=HIGHEST, preferred_element_type=jnp.float32) + jnp.dot(values[1], matrix[0].T, precision=HIGHEST, preferred_element_type=jnp.float32)
    return jnp.stack([real_part, imag_part])


def pair_apply(values, pos_a, pos_c, matrix):
    count_all = values.shape[1]
    lower_pos = min(pos_a, pos_c)
    upper_pos = max(pos_a, pos_c)
    shaped = values.reshape(2, count_all >> (upper_pos + 1), 2, 1 << (upper_pos - lower_pos - 1), 2, 1 << lower_pos)
    tensor = matrix.reshape(2, 2, 2, 2, 2)
    pattern = "uvwx,hwmxl->humvl" if pos_a < pos_c else "uvwx,hxmwl->hvmul"
    real_part = jnp.einsum(pattern, tensor[0], shaped[0], precision=HIGHEST) - jnp.einsum(pattern, tensor[1], shaped[1], precision=HIGHEST)
    imag_part = jnp.einsum(pattern, tensor[1], shaped[0], precision=HIGHEST) + jnp.einsum(pattern, tensor[0], shaped[1], precision=HIGHEST)
    return jnp.stack([real_part, imag_part]).reshape(2, count_all)


def spare_sign(count_all, spare_values):
    position = jnp.arange(count_all, dtype=jnp.int32)
    parity = jnp.zeros((count_all,), jnp.int32)
    for place_bit in range(spare_values.shape[0]):
        parity = parity + spare_values[place_bit] * (jnp.right_shift(position, place_bit) & 1)
    return (1 - 2 * (parity & 1)).astype(jnp.float32)


def reference(amplitudes, joined_gates, pair_gate, layout_in, layout_out, gate_qubits, spare_values):
    qubit_count = LQ + DQ + GQ
    flat_values = amplitudes.reshape(2, -1)
    qubit_ids = jnp.arange(qubit_count, dtype=jnp.int32)
    inverse_in = jnp.zeros((qubit_count,), jnp.int32).at[layout_in].set(qubit_ids)
    logical = jnp.take(flat_values, source_index(inverse_in, qubit_count), axis=1)
    for gate_num in range(GATES):
        chosen = gate_qubits[gate_num]
        member = qubit_ids[:, None] == chosen[None, :]
        inside = jnp.any(member, axis=1)
        others = jnp.logical_not(inside).astype(jnp.int32)
        inner_rank = jnp.sum(member * jnp.arange(chosen.shape[0], dtype=jnp.int32)[None, :], axis=1)
        target = jnp.where(inside, inner_rank, chosen.shape[0] + jnp.cumsum(others) - 1).astype(jnp.int32)
        bit_order = jnp.zeros((qubit_count,), jnp.int32).at[target].set(qubit_ids)
        arranged = jnp.take(logical, source_index(bit_order, qubit_count), axis=1)
        arranged = complex_gate(arranged.reshape(2, -1, SPAN), joined_gates[gate_num]).reshape(2, -1)
        logical = jnp.take(arranged, source_index(target, qubit_count), axis=1)
    stored = jnp.take(logical, source_index(layout_out, qubit_count), axis=1)
    stored = stored * spare_sign(stored.shape[1], spare_values)
    for bit_num in range(GQ):
        stored = pair_apply(stored, LQ + DQ + bit_num, LQ - 1 - bit_num, pair_gate)
    return stored.reshape(amplitudes.shape)
```

```python
import jax
import jax.numpy as jnp
from jax import lax
from jax.sharding import PartitionSpec as P

HIGHEST = lax.Precision.HIGHEST


def swapped(value, axis, bit):
    mask = 2**bit
    pairs = [(source, source ^ mask) for source in range(lax.axis_size(axis))]
    return lax.ppermute(value, axis, pairs)


def source_index(bit_order, bit_count):
    position = jnp.arange(2**bit_count, dtype=jnp.int32)
    source = jnp.zeros((2**bit_count,), jnp.int32)
    for place_bit in range(bit_count):
        source = source + jnp.left_shift(
            jnp.right_shift(position, place_bit) & 1, bit_order[place_bit]
        )
    return source


def reorder(values, source):
    bit_count = source.shape[0]
    length = 2**bit_count
    lane_bits = 7
    lanes = 2**lane_bits
    rows = length // lanes
    picked = source_index(source, bit_count)
    one_hot = (
        lax.broadcasted_iota(jnp.int32, (lanes, length), 0) == (picked & lanes - 1)[None, :]
    ).astype(jnp.float32)
    spread = jnp.dot(
        values.reshape(2 * rows, lanes),
        one_hot,
        precision=HIGHEST,
        preferred_element_type=jnp.float32,
    ).reshape(2, rows, length)
    row_hit = lax.broadcasted_iota(jnp.int32, (rows, length), 0) == jnp.right_shift(
        picked, lane_bits
    )[None, :]
    return jnp.sum(jnp.where(row_hit[None], spread, 0.0), axis=1)


def complex_gate(values, matrix):
    real_part = jnp.dot(
        values[0], matrix[0].T, precision=HIGHEST, preferred_element_type=jnp.float32
    ) - jnp.dot(values[1], matrix[1].T, precision=HIGHEST, preferred_element_type=jnp.float32)
    imag_part = jnp.dot(
        values[0], matrix[1].T, precision=HIGHEST, preferred_element_type=jnp.float32
    ) + jnp.dot(values[1], matrix[0].T, precision=HIGHEST, preferred_element_type=jnp.float32)
    return jnp.stack([real_part, imag_part])


def pair_apply(values, pos_a, pos_c, matrix):
    count_all = values.shape[1]
    lower_pos = min(pos_a, pos_c)
    upper_pos = max(pos_a, pos_c)
    shaped = values.reshape(
        2, count_all >> upper_pos + 1, 2, 1 << upper_pos - lower_pos - 1, 2, 1 << lower_pos
    )
    tensor = matrix.reshape(2, 2, 2, 2, 2)
    pattern = "uvwx,hwmxl->humvl"
    real_part = jnp.einsum(pattern, tensor[0], shaped[0], precision=HIGHEST) - jnp.einsum(
        pattern, tensor[1], shaped[1], precision=HIGHEST
    )
    imag_part = jnp.einsum(pattern, tensor[1], shaped[0], precision=HIGHEST) + jnp.einsum(
        pattern, tensor[0], shaped[1], precision=HIGHEST
    )
    return jnp.stack([real_part, imag_part]).reshape(2, count_all)


def spare_sign(count_all, spare_values):
    position = jnp.arange(count_all, dtype=jnp.int32)
    parity = jnp.zeros((count_all,), jnp.int32)
    for place_bit in range(spare_values.shape[0]):
        parity = parity + spare_values[place_bit] * (jnp.right_shift(position, place_bit) & 1)
    return (1 - 2 * (parity & 1)).astype(jnp.float32)


def position_of(layout, wanted):
    places = jnp.arange(layout.shape[0], dtype=jnp.int32)
    return jnp.sum(jnp.where(layout[None, :] == wanted[:, None], places[None, :], 0), axis=1)


def arrange(layout, leading, trailing):
    layout_len = layout.shape[0]
    lead_count = leading.shape[0]
    trail_count = trailing.shape[0]
    in_lead = layout[:, None] == leading[None, :]
    in_trail = layout[:, None] == trailing[None, :]
    lead_any = jnp.any(in_lead, axis=1)
    trail_any = jnp.any(in_trail, axis=1)
    remaining = jnp.logical_not(jnp.logical_or(lead_any, trail_any)).astype(jnp.int32)
    lead_rank = jnp.sum(in_lead * jnp.arange(lead_count, dtype=jnp.int32)[None, :], axis=1)
    trail_rank = (
        layout_len
        - trail_count
        + jnp.sum(in_trail * jnp.arange(trail_count, dtype=jnp.int32)[None, :], axis=1)
    )
    target = jnp.where(
        lead_any,
        lead_rank,
        jnp.where(trail_any, trail_rank, lead_count + jnp.cumsum(remaining) - 1),
    )
    places = jnp.arange(layout_len, dtype=jnp.int32)
    source = jnp.zeros((layout_len,), jnp.int32).at[target].set(places)
    new_layout = jnp.zeros((layout_len,), jnp.int32).at[target].set(layout)
    return (new_layout, source)


def halves(values, place_bit):
    count_all = values.shape[1]
    shaped = values.reshape(2, count_all >> place_bit + 1, 2, 1 << place_bit)
    return (shaped[:, :, 0], shaped[:, :, 1])


def rejoin(lower_half, upper_half, received, own_bit):
    keep_lower = own_bit == 0
    new_lower = jnp.where(keep_lower, lower_half, received)
    new_upper = jnp.where(keep_lower, received, upper_half)
    return jnp.stack([new_lower, new_upper], axis=2).reshape(2, -1)


def trade_group(values, place_bit, bit_num):
    lower_half, upper_half = halves(values, place_bit)
    own_bit = jnp.right_shift(lax.axis_index("grp"), bit_num) & 1
    outgoing = jnp.where(own_bit == 0, upper_half, lower_half)
    received = swapped(outgoing, "grp", bit_num)
    return rejoin(lower_half, upper_half, received, own_bit)


def pair_exchange(values, place_bit, bit_num, matrix):
    count_all = values.shape[1]
    own_bit = jnp.right_shift(lax.axis_index("grp"), bit_num) & 1
    received = swapped(values, "grp", bit_num)
    shape = (2, count_all >> place_bit + 1, 2, 1 << place_bit)
    own = values.reshape(shape)
    other = received.reshape(shape)
    same = jnp.where(own_bit == 0, matrix[:, 0::2, 0::2], matrix[:, 1::2, 1::2])
    cross = jnp.where(own_bit == 0, matrix[:, 0::2, 1::2], matrix[:, 1::2, 0::2])
    parts = []
    for out_c in range(2):
        real_part = 0.0
        imag_part = 0.0
        for in_c in range(2):
            for coef, src in ((same, own), (cross, other)):
                cr = coef[0, out_c, in_c]
                ci = coef[1, out_c, in_c]
                xr = src[0, :, in_c]
                xi = src[1, :, in_c]
                real_part = real_part + (cr * xr - ci * xi)
                imag_part = imag_part + (cr * xi + ci * xr)
        parts.append(jnp.stack([real_part, imag_part]))
    return jnp.stack(parts, axis=2).reshape(2, count_all)


def per_device(
    amplitudes, joined_gates, pair_gate, layout_in, layout_out, gate_qubits, spare_values
):
    length = amplitudes.shape[-1]
    local_bits = length.bit_length() - 1
    devices = lax.axis_size("dev")
    device_bits = devices.bit_length() - 1
    groups = lax.axis_size("grp")
    group_bits = groups.bit_length() - 1
    span_size = joined_gates.shape[-1]
    values = amplitudes.reshape(2, length)
    nothing = jnp.zeros((0,), jnp.int32)
    layout = layout_in[:local_bits]
    for gate_num in range(2):
        layout, source = arrange(layout, gate_qubits[gate_num], nothing)
        values = complex_gate(
            reorder(values, source).reshape(2, -1, span_size), joined_gates[gate_num]
        ).reshape(2, length)
    leaving = layout_out[local_bits : local_bits + device_bits]
    layout, source = arrange(layout, nothing, leaving)
    values = reorder(values, source)
    shaped = values.reshape(2, devices, length // devices)
    values = lax.all_to_all(shaped, "dev", split_axis=1, concat_axis=1, tiled=True).reshape(
        2, length
    )
    layout = jnp.concatenate(
        [layout[: local_bits - device_bits], layout_in[local_bits : local_bits + device_bits]]
    )
    for gate_num in range(2, 4):
        layout, source = arrange(layout, gate_qubits[gate_num], nothing)
        values = complex_gate(
            reorder(values, source).reshape(2, -1, span_size), joined_gates[gate_num]
        ).reshape(2, length)
    values = reorder(values, position_of(layout, layout_out[:local_bits]))
    values = values * spare_sign(length, spare_values)
    for bit_num in range(group_bits):
        values = pair_exchange(values, local_bits - 1 - bit_num, bit_num, pair_gate)
    return values.reshape(amplitudes.shape)


def solution(mesh):
    in_specs = (P(None, "grp", "dev", None), P(), P(), P(), P(), P(), P())
    out_specs = P(None, "grp", "dev", None)
    return jax.shard_map(
        per_device, mesh=mesh, in_specs=in_specs, out_specs=out_specs, check_vma=False
    )
```

```python
import jax
import jax.numpy as jnp
from jax import lax
from jax.sharding import PartitionSpec as P

HIGHEST = lax.Precision.HIGHEST


def swapped(value, axis, bit):
    mask = 2**bit
    pairs = [(source, source ^ mask) for source in range(lax.axis_size(axis))]
    return lax.ppermute(value, axis, pairs)


def source_index(bit_order, bit_count):
    position = jnp.arange(2**bit_count, dtype=jnp.int32)
    source = jnp.zeros((2**bit_count,), jnp.int32)
    for place_bit in range(bit_count):
        source = source + jnp.left_shift(
            jnp.right_shift(position, place_bit) & 1, bit_order[place_bit]
        )
    return source


def reorder(values, source):
    bit_count = source.shape[0]
    length = 2**bit_count
    lane_bits = 7
    lanes = 2**lane_bits
    rows = length // lanes
    picked = source_index(source, bit_count)
    one_hot = (
        lax.broadcasted_iota(jnp.int32, (lanes, length), 0) == (picked & lanes - 1)[None, :]
    ).astype(jnp.float32)
    spread = jnp.dot(
        values.reshape(2 * rows, lanes),
        one_hot,
        precision=HIGHEST,
        preferred_element_type=jnp.float32,
    ).reshape(2, rows, length)
    row_hit = lax.broadcasted_iota(jnp.int32, (rows, length), 0) == jnp.right_shift(
        picked, lane_bits
    )[None, :]
    return jnp.sum(jnp.where(row_hit[None], spread, 0.0), axis=1)


def complex_gate(values, matrix):
    real_part = jnp.dot(
        values[0], matrix[0].T, precision=HIGHEST, preferred_element_type=jnp.float32
    ) - jnp.dot(values[1], matrix[1].T, precision=HIGHEST, preferred_element_type=jnp.float32)
    imag_part = jnp.dot(
        values[0], matrix[1].T, precision=HIGHEST, preferred_element_type=jnp.float32
    ) + jnp.dot(values[1], matrix[0].T, precision=HIGHEST, preferred_element_type=jnp.float32)
    return jnp.stack([real_part, imag_part])


def pair_apply(values, pos_a, pos_c, matrix):
    count_all = values.shape[1]
    lower_pos = min(pos_a, pos_c)
    upper_pos = max(pos_a, pos_c)
    shaped = values.reshape(
        2, count_all >> upper_pos + 1, 2, 1 << upper_pos - lower_pos - 1, 2, 1 << lower_pos
    )
    tensor = matrix.reshape(2, 2, 2, 2, 2)
    pattern = "uvwx,hwmxl->humvl"
    real_part = jnp.einsum(pattern, tensor[0], shaped[0], precision=HIGHEST) - jnp.einsum(
        pattern, tensor[1], shaped[1], precision=HIGHEST
    )
    imag_part = jnp.einsum(pattern, tensor[1], shaped[0], precision=HIGHEST) + jnp.einsum(
        pattern, tensor[0], shaped[1], precision=HIGHEST
    )
    return jnp.stack([real_part, imag_part]).reshape(2, count_all)


def spare_sign(count_all, spare_values):
    lane_bits = 7
    lanes = 2**lane_bits
    rows = count_all // lanes
    lane_pos = jnp.arange(lanes, dtype=jnp.int32)
    row_pos = jnp.arange(rows, dtype=jnp.int32)
    lane_parity = jnp.zeros((lanes,), jnp.int32)
    row_parity = jnp.zeros((rows,), jnp.int32)
    for place_bit in range(spare_values.shape[0]):
        if place_bit < lane_bits:
            lane_parity = lane_parity + spare_values[place_bit] * (
                jnp.right_shift(lane_pos, place_bit) & 1
            )
        else:
            row_parity = row_parity + spare_values[place_bit] * (
                jnp.right_shift(row_pos, place_bit - lane_bits) & 1
            )
    parity = row_parity[:, None] + lane_parity[None, :]
    return (1 - 2 * (parity & 1)).astype(jnp.float32).reshape(count_all)


def position_of(layout, wanted):
    places = jnp.arange(layout.shape[0], dtype=jnp.int32)
    return jnp.sum(jnp.where(layout[None, :] == wanted[:, None], places[None, :], 0), axis=1)


def arrange(layout, leading, trailing):
    layout_len = layout.shape[0]
    lead_count = leading.shape[0]
    trail_count = trailing.shape[0]
    in_lead = layout[:, None] == leading[None, :]
    in_trail = layout[:, None] == trailing[None, :]
    lead_any = jnp.any(in_lead, axis=1)
    trail_any = jnp.any(in_trail, axis=1)
    remaining = jnp.logical_not(jnp.logical_or(lead_any, trail_any)).astype(jnp.int32)
    lead_rank = jnp.sum(in_lead * jnp.arange(lead_count, dtype=jnp.int32)[None, :], axis=1)
    trail_rank = (
        layout_len
        - trail_count
        + jnp.sum(in_trail * jnp.arange(trail_count, dtype=jnp.int32)[None, :], axis=1)
    )
    target = jnp.where(
        lead_any,
        lead_rank,
        jnp.where(trail_any, trail_rank, lead_count + jnp.cumsum(remaining) - 1),
    )
    places = jnp.arange(layout_len, dtype=jnp.int32)
    source = jnp.zeros((layout_len,), jnp.int32).at[target].set(places)
    new_layout = jnp.zeros((layout_len,), jnp.int32).at[target].set(layout)
    return (new_layout, source)


def halves(values, place_bit):
    count_all = values.shape[1]
    shaped = values.reshape(2, count_all >> place_bit + 1, 2, 1 << place_bit)
    return (shaped[:, :, 0], shaped[:, :, 1])


def rejoin(lower_half, upper_half, received, own_bit):
    keep_lower = own_bit == 0
    new_lower = jnp.where(keep_lower, lower_half, received)
    new_upper = jnp.where(keep_lower, received, upper_half)
    return jnp.stack([new_lower, new_upper], axis=2).reshape(2, -1)


def trade_group(values, place_bit, bit_num):
    lower_half, upper_half = halves(values, place_bit)
    own_bit = jnp.right_shift(lax.axis_index("grp"), bit_num) & 1
    outgoing = jnp.where(own_bit == 0, upper_half, lower_half)
    received = swapped(outgoing, "grp", bit_num)
    return rejoin(lower_half, upper_half, received, own_bit)


def pair_exchange(values, place_bit, bit_num, matrix):
    count_all = values.shape[1]
    own_bit = jnp.right_shift(lax.axis_index("grp"), bit_num) & 1
    received = swapped(values, "grp", bit_num)
    shape = (2, count_all >> place_bit + 1, 2, 1 << place_bit)
    own = values.reshape(shape)
    other = received.reshape(shape)
    same = jnp.where(own_bit == 0, matrix[:, 0::2, 0::2], matrix[:, 1::2, 1::2])
    cross = jnp.where(own_bit == 0, matrix[:, 0::2, 1::2], matrix[:, 1::2, 0::2])
    parts = []
    for out_c in range(2):
        real_part = 0.0
        imag_part = 0.0
        for in_c in range(2):
            for coef, src in ((same, own), (cross, other)):
                cr = coef[0, out_c, in_c]
                ci = coef[1, out_c, in_c]
                xr = src[0, :, in_c]
                xi = src[1, :, in_c]
                real_part = real_part + (cr * xr - ci * xi)
                imag_part = imag_part + (cr * xi + ci * xr)
        parts.append(jnp.stack([real_part, imag_part]))
    return jnp.stack(parts, axis=2).reshape(2, count_all)


def pair_operator(matrix, group_bits):
    size = 2 ** (2 * group_bits)
    place = jnp.arange(size, dtype=jnp.int32)
    states = jnp.arange(4, dtype=jnp.int32)
    real_part = None
    imag_part = None
    for bit_num in range(group_bits):
        pair_state = (jnp.right_shift(place, bit_num) & 1) + 2 * (
            jnp.right_shift(place, 2 * group_bits - 1 - bit_num) & 1
        )
        pick = (pair_state[:, None] == states[None, :]).astype(jnp.float32)
        factor_re = jnp.dot(
            jnp.dot(pick, matrix[0], precision=HIGHEST), pick.T, precision=HIGHEST
        )
        factor_im = jnp.dot(
            jnp.dot(pick, matrix[1], precision=HIGHEST), pick.T, precision=HIGHEST
        )
        if real_part is None:
            real_part, imag_part = factor_re, factor_im
        else:
            real_part, imag_part = (
                real_part * factor_re - imag_part * factor_im,
                real_part * factor_im + imag_part * factor_re,
            )
    return (real_part, imag_part)


def group_gates(values, local_bits, group_bits, matrix):
    length = values.shape[1]
    groups = 2**group_bits
    low = local_bits - 2 * group_bits
    shaped = values.reshape(2, groups, groups, 2**low)
    shaped = lax.all_to_all(shaped, "grp", split_axis=2, concat_axis=2, tiled=True)
    real_op, imag_op = pair_operator(matrix, group_bits)
    block = shaped.reshape(2, groups * groups, 2**low)
    real_part = jnp.dot(
        real_op, block[0], precision=HIGHEST, preferred_element_type=jnp.float32
    ) - jnp.dot(imag_op, block[1], precision=HIGHEST, preferred_element_type=jnp.float32)
    imag_part = jnp.dot(
        real_op, block[1], precision=HIGHEST, preferred_element_type=jnp.float32
    ) + jnp.dot(imag_op, block[0], precision=HIGHEST, preferred_element_type=jnp.float32)
    shaped = jnp.stack([real_part, imag_part]).reshape(2, groups, groups, 2**low)
    shaped = lax.all_to_all(shaped, "grp", split_axis=2, concat_axis=2, tiled=True)
    return shaped.reshape(2, length)


def per_device(
    amplitudes, joined_gates, pair_gate, layout_in, layout_out, gate_qubits, spare_values
):
    length = amplitudes.shape[-1]
    local_bits = length.bit_length() - 1
    devices = lax.axis_size("dev")
    device_bits = devices.bit_length() - 1
    groups = lax.axis_size("grp")
    group_bits = groups.bit_length() - 1
    span_size = joined_gates.shape[-1]
    values = amplitudes.reshape(2, length)
    nothing = jnp.zeros((0,), jnp.int32)
    layout = layout_in[:local_bits]
    for gate_num in range(2):
        layout, source = arrange(layout, gate_qubits[gate_num], nothing)
        values = complex_gate(
            reorder(values, source).reshape(2, -1, span_size), joined_gates[gate_num]
        ).reshape(2, length)
    leaving = layout_out[local_bits : local_bits + device_bits]
    layout, source = arrange(layout, nothing, leaving)
    values = reorder(values, source)
    shaped = values.reshape(2, devices, length // devices)
    values = lax.all_to_all(shaped, "dev", split_axis=1, concat_axis=1, tiled=True).reshape(
        2, length
    )
    layout = jnp.concatenate(
        [layout[: local_bits - device_bits], layout_in[local_bits : local_bits + device_bits]]
    )
    for gate_num in range(2, 4):
        layout, source = arrange(layout, gate_qubits[gate_num], nothing)
        values = complex_gate(
            reorder(values, source).reshape(2, -1, span_size), joined_gates[gate_num]
        ).reshape(2, length)
    values = reorder(values, position_of(layout, layout_out[:local_bits]))
    values = values * spare_sign(length, spare_values)
    values = group_gates(values, local_bits, group_bits, pair_gate)
    return values.reshape(amplitudes.shape)


def solution(mesh):
    in_specs = (P(None, "grp", "dev", None), P(), P(), P(), P(), P(), P())
    out_specs = P(None, "grp", "dev", None)
    return jax.shard_map(
        per_device, mesh=mesh, in_specs=in_specs, out_specs=out_specs, check_vma=False
    )
```

```python
import jax
import jax.numpy as jnp
from jax import lax
from jax.sharding import PartitionSpec as P

HIGHEST = lax.Precision.HIGHEST


def swapped(value, axis, bit):
    mask = 2**bit
    pairs = [(source, source ^ mask) for source in range(lax.axis_size(axis))]
    return lax.ppermute(value, axis, pairs)


def source_index(bit_order, bit_count):
    position = jnp.arange(2**bit_count, dtype=jnp.int32)
    source = jnp.zeros((2**bit_count,), jnp.int32)
    for place_bit in range(bit_count):
        source = source + jnp.left_shift(
            jnp.right_shift(position, place_bit) & 1, bit_order[place_bit]
        )
    return source


def reorder(values, source):
    bit_count = source.shape[0]
    length = 2**bit_count
    lane_bits = 7
    lanes = 2**lane_bits
    rows = length // lanes
    picked = source_index(source, bit_count)
    one_hot = (
        lax.broadcasted_iota(jnp.int32, (lanes, length), 0) == (picked & lanes - 1)[None, :]
    ).astype(jnp.float32)
    spread = jnp.dot(
        values.reshape(2 * rows, lanes),
        one_hot,
        precision=HIGHEST,
        preferred_element_type=jnp.float32,
    ).reshape(2, rows, length)
    row_hit = lax.broadcasted_iota(jnp.int32, (rows, length), 0) == jnp.right_shift(
        picked, lane_bits
    )[None, :]
    return jnp.sum(jnp.where(row_hit[None], spread, 0.0), axis=1)


def complex_gate(values, matrix):
    real_part = jnp.dot(
        values[0], matrix[0].T, precision=HIGHEST, preferred_element_type=jnp.float32
    ) - jnp.dot(values[1], matrix[1].T, precision=HIGHEST, preferred_element_type=jnp.float32)
    imag_part = jnp.dot(
        values[0], matrix[1].T, precision=HIGHEST, preferred_element_type=jnp.float32
    ) + jnp.dot(values[1], matrix[0].T, precision=HIGHEST, preferred_element_type=jnp.float32)
    return jnp.stack([real_part, imag_part])


def pair_apply(values, pos_a, pos_c, matrix):
    count_all = values.shape[1]
    lower_pos = min(pos_a, pos_c)
    upper_pos = max(pos_a, pos_c)
    shaped = values.reshape(
        2, count_all >> upper_pos + 1, 2, 1 << upper_pos - lower_pos - 1, 2, 1 << lower_pos
    )
    tensor = matrix.reshape(2, 2, 2, 2, 2)
    pattern = "uvwx,hwmxl->humvl"
    real_part = jnp.einsum(pattern, tensor[0], shaped[0], precision=HIGHEST) - jnp.einsum(
        pattern, tensor[1], shaped[1], precision=HIGHEST
    )
    imag_part = jnp.einsum(pattern, tensor[1], shaped[0], precision=HIGHEST) + jnp.einsum(
        pattern, tensor[0], shaped[1], precision=HIGHEST
    )
    return jnp.stack([real_part, imag_part]).reshape(2, count_all)


def spare_sign(count_all, spare_values):
    lane_bits = 7
    lanes = 2**lane_bits
    rows = count_all // lanes
    lane_pos = jnp.arange(lanes, dtype=jnp.int32)
    row_pos = jnp.arange(rows, dtype=jnp.int32)
    lane_parity = jnp.zeros((lanes,), jnp.int32)
    row_parity = jnp.zeros((rows,), jnp.int32)
    for place_bit in range(spare_values.shape[0]):
        if place_bit < lane_bits:
            lane_parity = lane_parity + spare_values[place_bit] * (
                jnp.right_shift(lane_pos, place_bit) & 1
            )
        else:
            row_parity = row_parity + spare_values[place_bit] * (
                jnp.right_shift(row_pos, place_bit - lane_bits) & 1
            )
    parity = row_parity[:, None] + lane_parity[None, :]
    return (1 - 2 * (parity & 1)).astype(jnp.float32).reshape(count_all)


def position_of(layout, wanted):
    places = jnp.arange(layout.shape[0], dtype=jnp.int32)
    return jnp.sum(jnp.where(layout[None, :] == wanted[:, None], places[None, :], 0), axis=1)


def arrange(layout, leading, trailing):
    layout_len = layout.shape[0]
    lead_count = leading.shape[0]
    trail_count = trailing.shape[0]
    in_lead = layout[:, None] == leading[None, :]
    in_trail = layout[:, None] == trailing[None, :]
    lead_any = jnp.any(in_lead, axis=1)
    trail_any = jnp.any(in_trail, axis=1)
    remaining = jnp.logical_not(jnp.logical_or(lead_any, trail_any)).astype(jnp.int32)
    lead_rank = jnp.sum(in_lead * jnp.arange(lead_count, dtype=jnp.int32)[None, :], axis=1)
    trail_rank = (
        layout_len
        - trail_count
        + jnp.sum(in_trail * jnp.arange(trail_count, dtype=jnp.int32)[None, :], axis=1)
    )
    target = jnp.where(
        lead_any,
        lead_rank,
        jnp.where(trail_any, trail_rank, lead_count + jnp.cumsum(remaining) - 1),
    )
    places = jnp.arange(layout_len, dtype=jnp.int32)
    source = jnp.zeros((layout_len,), jnp.int32).at[target].set(places)
    new_layout = jnp.zeros((layout_len,), jnp.int32).at[target].set(layout)
    return (new_layout, source)


def halves(values, place_bit):
    count_all = values.shape[1]
    shaped = values.reshape(2, count_all >> place_bit + 1, 2, 1 << place_bit)
    return (shaped[:, :, 0], shaped[:, :, 1])


def rejoin(lower_half, upper_half, received, own_bit):
    keep_lower = own_bit == 0
    new_lower = jnp.where(keep_lower, lower_half, received)
    new_upper = jnp.where(keep_lower, received, upper_half)
    return jnp.stack([new_lower, new_upper], axis=2).reshape(2, -1)


def trade_group(values, place_bit, bit_num):
    lower_half, upper_half = halves(values, place_bit)
    own_bit = jnp.right_shift(lax.axis_index("grp"), bit_num) & 1
    outgoing = jnp.where(own_bit == 0, upper_half, lower_half)
    received = swapped(outgoing, "grp", bit_num)
    return rejoin(lower_half, upper_half, received, own_bit)


def pair_exchange(values, place_bit, bit_num, matrix):
    length = values.shape[1]
    lane_bits = 7
    rows = length >> lane_bits
    row_bit = place_bit - lane_bits
    own_bit = jnp.right_shift(lax.axis_index("grp"), bit_num) & 1
    received = swapped(values, "grp", bit_num)
    place = jnp.arange(rows, dtype=jnp.int32)
    mask = 1 << row_bit
    agree = (place[:, None] | mask) == (place[None, :] | mask)
    pair_bit = jnp.right_shift(place, row_bit) & 1
    states = jnp.arange(4, dtype=jnp.int32)
    pick_out = ((own_bit + 2 * pair_bit)[:, None] == states[None, :]).astype(jnp.float32)
    pick_par = ((1 - own_bit + 2 * pair_bit)[:, None] == states[None, :]).astype(jnp.float32)
    blocks = []
    for pick_in in (pick_out, pick_par):
        for part in range(2):
            coef = jnp.dot(
                jnp.dot(pick_out, matrix[part], precision=HIGHEST), pick_in.T, precision=HIGHEST
            )
            blocks.append(jnp.where(agree, coef, 0.0))
    own_re, own_im, par_re, par_im = blocks
    operator = jnp.concatenate(
        [
            jnp.concatenate([own_re, -own_im, par_re, -par_im], axis=1),
            jnp.concatenate([own_im, own_re, par_im, par_re], axis=1),
        ],
        axis=0,
    )
    stacked = jnp.concatenate(
        [values.reshape(2 * rows, -1), received.reshape(2 * rows, -1)], axis=0
    )
    out = jnp.dot(operator, stacked, precision=HIGHEST, preferred_element_type=jnp.float32)
    return out.reshape(2, length)


def pair_operator(matrix, group_bits):
    size = 2 ** (2 * group_bits)
    place = jnp.arange(size, dtype=jnp.int32)
    states = jnp.arange(4, dtype=jnp.int32)
    real_part = None
    imag_part = None
    for bit_num in range(group_bits):
        pair_state = (jnp.right_shift(place, bit_num) & 1) + 2 * (
            jnp.right_shift(place, 2 * group_bits - 1 - bit_num) & 1
        )
        pick = (pair_state[:, None] == states[None, :]).astype(jnp.float32)
        factor_re = jnp.dot(
            jnp.dot(pick, matrix[0], precision=HIGHEST), pick.T, precision=HIGHEST
        )
        factor_im = jnp.dot(
            jnp.dot(pick, matrix[1], precision=HIGHEST), pick.T, precision=HIGHEST
        )
        if real_part is None:
            real_part, imag_part = factor_re, factor_im
        else:
            real_part, imag_part = (
                real_part * factor_re - imag_part * factor_im,
                real_part * factor_im + imag_part * factor_re,
            )
    return (real_part, imag_part)


def group_gates(values, local_bits, group_bits, matrix):
    length = values.shape[1]
    groups = 2**group_bits
    low = local_bits - 2 * group_bits
    shaped = values.reshape(2, groups, groups, 2**low)
    shaped = lax.all_to_all(shaped, "grp", split_axis=2, concat_axis=2, tiled=True)
    real_op, imag_op = pair_operator(matrix, group_bits)
    block = shaped.reshape(2, groups * groups, 2**low)
    real_part = jnp.dot(
        real_op, block[0], precision=HIGHEST, preferred_element_type=jnp.float32
    ) - jnp.dot(imag_op, block[1], precision=HIGHEST, preferred_element_type=jnp.float32)
    imag_part = jnp.dot(
        real_op, block[1], precision=HIGHEST, preferred_element_type=jnp.float32
    ) + jnp.dot(imag_op, block[0], precision=HIGHEST, preferred_element_type=jnp.float32)
    shaped = jnp.stack([real_part, imag_part]).reshape(2, groups, groups, 2**low)
    shaped = lax.all_to_all(shaped, "grp", split_axis=2, concat_axis=2, tiled=True)
    return shaped.reshape(2, length)


def per_device(
    amplitudes, joined_gates, pair_gate, layout_in, layout_out, gate_qubits, spare_values
):
    length = amplitudes.shape[-1]
    local_bits = length.bit_length() - 1
    devices = lax.axis_size("dev")
    device_bits = devices.bit_length() - 1
    groups = lax.axis_size("grp")
    group_bits = groups.bit_length() - 1
    span_size = joined_gates.shape[-1]
    values = amplitudes.reshape(2, length)
    nothing = jnp.zeros((0,), jnp.int32)
    layout = layout_in[:local_bits]
    for gate_num in range(2):
        layout, source = arrange(layout, gate_qubits[gate_num], nothing)
        values = complex_gate(
            reorder(values, source).reshape(2, -1, span_size), joined_gates[gate_num]
        ).reshape(2, length)
    leaving = layout_out[local_bits : local_bits + device_bits]
    layout, source = arrange(layout, nothing, leaving)
    values = reorder(values, source)
    shaped = values.reshape(2, devices, length // devices)
    values = lax.all_to_all(shaped, "dev", split_axis=1, concat_axis=1, tiled=True).reshape(
        2, length
    )
    layout = jnp.concatenate(
        [layout[: local_bits - device_bits], layout_in[local_bits : local_bits + device_bits]]
    )
    for gate_num in range(2, 4):
        layout, source = arrange(layout, gate_qubits[gate_num], nothing)
        values = complex_gate(
            reorder(values, source).reshape(2, -1, span_size), joined_gates[gate_num]
        ).reshape(2, length)
    values = reorder(values, position_of(layout, layout_out[:local_bits]))
    values = values * spare_sign(length, spare_values)
    for bit_num in range(group_bits):
        values = pair_exchange(values, local_bits - 1 - bit_num, bit_num, pair_gate)
    return values.reshape(amplitudes.shape)


def solution(mesh):
    in_specs = (P(None, "grp", "dev", None), P(), P(), P(), P(), P(), P())
    out_specs = P(None, "grp", "dev", None)
    return jax.shard_map(
        per_device, mesh=mesh, in_specs=in_specs, out_specs=out_specs, check_vma=False
    )
```

```python
import jax
import jax.numpy as jnp
from jax import lax
from jax.sharding import PartitionSpec as P

HIGHEST = lax.Precision.HIGHEST


def swapped(value, axis, bit):
    mask = 2**bit
    pairs = [(source, source ^ mask) for source in range(lax.axis_size(axis))]
    return lax.ppermute(value, axis, pairs)


def bit_table(bit_count):
    place = jnp.arange(2**bit_count, dtype=jnp.int32)[:, None]
    return jnp.right_shift(place, jnp.arange(bit_count, dtype=jnp.int32)[None, :]) & 1


def source_index(bit_order, bit_count):
    lane_bits = min(7, bit_count)
    lane_part = jnp.sum(
        jnp.left_shift(bit_table(lane_bits), bit_order[None, :lane_bits]), axis=1
    )
    row_part = jnp.sum(
        jnp.left_shift(bit_table(bit_count - lane_bits), bit_order[None, lane_bits:]), axis=1
    )
    return (row_part[:, None] + lane_part[None, :]).reshape(2**bit_count)


def reorder(values, source):
    bit_count = source.shape[0]
    length = 2**bit_count
    lane_bits = 7
    lanes = 2**lane_bits
    rows = length // lanes
    picked = source_index(source, bit_count)
    one_hot = (
        lax.broadcasted_iota(jnp.int32, (lanes, length), 0) == (picked & lanes - 1)[None, :]
    ).astype(jnp.float32)
    spread = jnp.dot(
        values.reshape(2 * rows, lanes),
        one_hot,
        precision=HIGHEST,
        preferred_element_type=jnp.float32,
    ).reshape(2, rows, length)
    row_hit = lax.broadcasted_iota(jnp.int32, (rows, length), 0) == jnp.right_shift(
        picked, lane_bits
    )[None, :]
    return jnp.sum(jnp.where(row_hit[None], spread, 0.0), axis=1)


def complex_gate(values, matrix):
    real_part = jnp.dot(
        values[0], matrix[0].T, precision=HIGHEST, preferred_element_type=jnp.float32
    ) - jnp.dot(values[1], matrix[1].T, precision=HIGHEST, preferred_element_type=jnp.float32)
    imag_part = jnp.dot(
        values[0], matrix[1].T, precision=HIGHEST, preferred_element_type=jnp.float32
    ) + jnp.dot(values[1], matrix[0].T, precision=HIGHEST, preferred_element_type=jnp.float32)
    return jnp.stack([real_part, imag_part])


def pair_apply(values, pos_a, pos_c, matrix):
    count_all = values.shape[1]
    lower_pos = min(pos_a, pos_c)
    upper_pos = max(pos_a, pos_c)
    shaped = values.reshape(
        2, count_all >> upper_pos + 1, 2, 1 << upper_pos - lower_pos - 1, 2, 1 << lower_pos
    )
    tensor = matrix.reshape(2, 2, 2, 2, 2)
    pattern = "uvwx,hwmxl->humvl"
    real_part = jnp.einsum(pattern, tensor[0], shaped[0], precision=HIGHEST) - jnp.einsum(
        pattern, tensor[1], shaped[1], precision=HIGHEST
    )
    imag_part = jnp.einsum(pattern, tensor[1], shaped[0], precision=HIGHEST) + jnp.einsum(
        pattern, tensor[0], shaped[1], precision=HIGHEST
    )
    return jnp.stack([real_part, imag_part]).reshape(2, count_all)


def spare_sign(count_all, spare_values):
    lane_bits = 7
    spare_count = spare_values.shape[0]
    row_bits = spare_count - lane_bits
    lane_parity = jnp.sum(bit_table(lane_bits) * spare_values[None, :lane_bits], axis=1)
    row_parity = jnp.sum(bit_table(row_bits) * spare_values[None, lane_bits:], axis=1)
    repeat = count_all // (2**spare_count)
    parity = row_parity[:, None] + lane_parity[None, :]
    sign = (1 - 2 * (parity & 1)).astype(jnp.float32).reshape(1, 2**spare_count)
    return jnp.broadcast_to(sign, (repeat, 2**spare_count)).reshape(count_all)


def position_of(layout, wanted):
    places = jnp.arange(layout.shape[0], dtype=jnp.int32)
    return jnp.sum(jnp.where(layout[None, :] == wanted[:, None], places[None, :], 0), axis=1)


def arrange(layout, leading, trailing):
    layout_len = layout.shape[0]
    lead_count = leading.shape[0]
    trail_count = trailing.shape[0]
    in_lead = layout[:, None] == leading[None, :]
    in_trail = layout[:, None] == trailing[None, :]
    lead_any = jnp.any(in_lead, axis=1)
    trail_any = jnp.any(in_trail, axis=1)
    remaining = jnp.logical_not(jnp.logical_or(lead_any, trail_any)).astype(jnp.int32)
    lead_rank = jnp.sum(in_lead * jnp.arange(lead_count, dtype=jnp.int32)[None, :], axis=1)
    trail_rank = (
        layout_len
        - trail_count
        + jnp.sum(in_trail * jnp.arange(trail_count, dtype=jnp.int32)[None, :], axis=1)
    )
    target = jnp.where(
        lead_any,
        lead_rank,
        jnp.where(trail_any, trail_rank, lead_count + jnp.cumsum(remaining) - 1),
    )
    places = jnp.arange(layout_len, dtype=jnp.int32)
    lands = target[None, :] == places[:, None]
    source = jnp.sum(jnp.where(lands, places[None, :], 0), axis=1)
    new_layout = jnp.sum(jnp.where(lands, layout[None, :], 0), axis=1)
    return (new_layout, source)


def halves(values, place_bit):
    count_all = values.shape[1]
    shaped = values.reshape(2, count_all >> place_bit + 1, 2, 1 << place_bit)
    return (shaped[:, :, 0], shaped[:, :, 1])


def rejoin(lower_half, upper_half, received, own_bit):
    keep_lower = own_bit == 0
    new_lower = jnp.where(keep_lower, lower_half, received)
    new_upper = jnp.where(keep_lower, received, upper_half)
    return jnp.stack([new_lower, new_upper], axis=2).reshape(2, -1)


def trade_group(values, place_bit, bit_num):
    lower_half, upper_half = halves(values, place_bit)
    own_bit = jnp.right_shift(lax.axis_index("grp"), bit_num) & 1
    outgoing = jnp.where(own_bit == 0, upper_half, lower_half)
    received = swapped(outgoing, "grp", bit_num)
    return rejoin(lower_half, upper_half, received, own_bit)


def pair_exchange(values, place_bit, bit_num, matrix):
    length = values.shape[1]
    lane_bits = 7
    rows = length >> lane_bits
    row_bit = place_bit - lane_bits
    own_bit = jnp.right_shift(lax.axis_index("grp"), bit_num) & 1
    received = swapped(values, "grp", bit_num)
    place = jnp.arange(rows, dtype=jnp.int32)
    mask = 1 << row_bit
    agree = (place[:, None] | mask) == (place[None, :] | mask)
    pair_bit = jnp.right_shift(place, row_bit) & 1
    states = jnp.arange(4, dtype=jnp.int32)
    pick_out = ((own_bit + 2 * pair_bit)[:, None] == states[None, :]).astype(jnp.float32)
    pick_par = ((1 - own_bit + 2 * pair_bit)[:, None] == states[None, :]).astype(jnp.float32)
    blocks = []
    for pick_in in (pick_out, pick_par):
        for part in range(2):
            coef = jnp.dot(
                jnp.dot(pick_out, matrix[part], precision=HIGHEST), pick_in.T, precision=HIGHEST
            )
            blocks.append(jnp.where(agree, coef, 0.0))
    own_re, own_im, par_re, par_im = blocks
    operator = jnp.concatenate(
        [
            jnp.concatenate([own_re, -own_im, par_re, -par_im], axis=1),
            jnp.concatenate([own_im, own_re, par_im, par_re], axis=1),
        ],
        axis=0,
    )
    stacked = jnp.concatenate(
        [values.reshape(2 * rows, -1), received.reshape(2 * rows, -1)], axis=0
    )
    out = jnp.dot(operator, stacked, precision=HIGHEST, preferred_element_type=jnp.float32)
    return out.reshape(2, length)


def pair_operator(matrix, group_bits):
    size = 2 ** (2 * group_bits)
    place = jnp.arange(size, dtype=jnp.int32)
    states = jnp.arange(4, dtype=jnp.int32)
    real_part = None
    imag_part = None
    for bit_num in range(group_bits):
        pair_state = (jnp.right_shift(place, bit_num) & 1) + 2 * (
            jnp.right_shift(place, 2 * group_bits - 1 - bit_num) & 1
        )
        pick = (pair_state[:, None] == states[None, :]).astype(jnp.float32)
        factor_re = jnp.dot(
            jnp.dot(pick, matrix[0], precision=HIGHEST), pick.T, precision=HIGHEST
        )
        factor_im = jnp.dot(
            jnp.dot(pick, matrix[1], precision=HIGHEST), pick.T, precision=HIGHEST
        )
        if real_part is None:
            real_part, imag_part = factor_re, factor_im
        else:
            real_part, imag_part = (
                real_part * factor_re - imag_part * factor_im,
                real_part * factor_im + imag_part * factor_re,
            )
    return (real_part, imag_part)


def group_gates(values, local_bits, group_bits, matrix):
    length = values.shape[1]
    groups = 2**group_bits
    low = local_bits - 2 * group_bits
    shaped = values.reshape(2, groups, groups, 2**low)
    shaped = lax.all_to_all(shaped, "grp", split_axis=2, concat_axis=2, tiled=True)
    real_op, imag_op = pair_operator(matrix, group_bits)
    block = shaped.reshape(2, groups * groups, 2**low)
    real_part = jnp.dot(
        real_op, block[0], precision=HIGHEST, preferred_element_type=jnp.float32
    ) - jnp.dot(imag_op, block[1], precision=HIGHEST, preferred_element_type=jnp.float32)
    imag_part = jnp.dot(
        real_op, block[1], precision=HIGHEST, preferred_element_type=jnp.float32
    ) + jnp.dot(imag_op, block[0], precision=HIGHEST, preferred_element_type=jnp.float32)
    shaped = jnp.stack([real_part, imag_part]).reshape(2, groups, groups, 2**low)
    shaped = lax.all_to_all(shaped, "grp", split_axis=2, concat_axis=2, tiled=True)
    return shaped.reshape(2, length)


def per_device(
    amplitudes, joined_gates, pair_gate, layout_in, layout_out, gate_qubits, spare_values
):
    length = amplitudes.shape[-1]
    local_bits = length.bit_length() - 1
    devices = lax.axis_size("dev")
    device_bits = devices.bit_length() - 1
    groups = lax.axis_size("grp")
    group_bits = groups.bit_length() - 1
    span_size = joined_gates.shape[-1]
    values = amplitudes.reshape(2, length)
    nothing = jnp.zeros((0,), jnp.int32)
    layout = layout_in[:local_bits]
    for gate_num in range(2):
        layout, source = arrange(layout, gate_qubits[gate_num], nothing)
        values = complex_gate(
            reorder(values, source).reshape(2, -1, span_size), joined_gates[gate_num]
        ).reshape(2, length)
    leaving = layout_out[local_bits : local_bits + device_bits]
    layout, source = arrange(layout, nothing, leaving)
    values = reorder(values, source)
    shaped = values.reshape(2, devices, length // devices)
    values = lax.all_to_all(shaped, "dev", split_axis=1, concat_axis=1, tiled=True).reshape(
        2, length
    )
    layout = jnp.concatenate(
        [layout[: local_bits - device_bits], layout_in[local_bits : local_bits + device_bits]]
    )
    for gate_num in range(2, 4):
        layout, source = arrange(layout, gate_qubits[gate_num], nothing)
        values = complex_gate(
            reorder(values, source).reshape(2, -1, span_size), joined_gates[gate_num]
        ).reshape(2, length)
    values = reorder(values, position_of(layout, layout_out[:local_bits]))
    values = values * spare_sign(length, spare_values)
    for bit_num in range(group_bits):
        values = pair_exchange(values, local_bits - 1 - bit_num, bit_num, pair_gate)
    return values.reshape(amplitudes.shape)


def solution(mesh):
    in_specs = (P(None, "grp", "dev", None), P(), P(), P(), P(), P(), P())
    out_specs = P(None, "grp", "dev", None)
    return jax.shard_map(
        per_device, mesh=mesh, in_specs=in_specs, out_specs=out_specs, check_vma=False
    )
```

```python
import jax
import jax.numpy as jnp
from jax import lax
from jax.sharding import PartitionSpec as P

HIGHEST = lax.Precision.HIGHEST


def swapped(value, axis, bit):
    mask = 2**bit
    pairs = [(source, source ^ mask) for source in range(lax.axis_size(axis))]
    return lax.ppermute(value, axis, pairs)


def bit_table(bit_count):
    place = jnp.arange(2**bit_count, dtype=jnp.int32)[:, None]
    return jnp.right_shift(place, jnp.arange(bit_count, dtype=jnp.int32)[None, :]) & 1


def source_index(bit_order, bit_count):
    lane_bits = min(7, bit_count)
    lane_part = jnp.sum(
        jnp.left_shift(bit_table(lane_bits), bit_order[None, :lane_bits]), axis=1
    )
    row_part = jnp.sum(
        jnp.left_shift(bit_table(bit_count - lane_bits), bit_order[None, lane_bits:]), axis=1
    )
    return (row_part[:, None] + lane_part[None, :]).reshape(2**bit_count)


def reorder(values, source):
    bit_count = source.shape[0]
    length = 2**bit_count
    lane_bits = 7
    lanes = 2**lane_bits
    rows = length // lanes
    picked = source_index(source, bit_count)
    one_hot = (
        lax.broadcasted_iota(jnp.int32, (lanes, length), 0) == (picked & lanes - 1)[None, :]
    ).astype(jnp.float32)
    spread = jnp.dot(
        values.reshape(2 * rows, lanes),
        one_hot,
        precision=HIGHEST,
        preferred_element_type=jnp.float32,
    ).reshape(2, rows, length)
    row_hit = lax.broadcasted_iota(jnp.int32, (rows, length), 0) == jnp.right_shift(
        picked, lane_bits
    )[None, :]
    return jnp.sum(jnp.where(row_hit[None], spread, 0.0), axis=1)


def complex_gate(values, matrix):
    real_part = jnp.dot(
        values[0], matrix[0].T, precision=HIGHEST, preferred_element_type=jnp.float32
    ) - jnp.dot(values[1], matrix[1].T, precision=HIGHEST, preferred_element_type=jnp.float32)
    imag_part = jnp.dot(
        values[0], matrix[1].T, precision=HIGHEST, preferred_element_type=jnp.float32
    ) + jnp.dot(values[1], matrix[0].T, precision=HIGHEST, preferred_element_type=jnp.float32)
    return jnp.stack([real_part, imag_part])


def pair_apply(values, pos_a, pos_c, matrix):
    count_all = values.shape[1]
    lower_pos = min(pos_a, pos_c)
    upper_pos = max(pos_a, pos_c)
    shaped = values.reshape(
        2, count_all >> upper_pos + 1, 2, 1 << upper_pos - lower_pos - 1, 2, 1 << lower_pos
    )
    tensor = matrix.reshape(2, 2, 2, 2, 2)
    pattern = "uvwx,hwmxl->humvl"
    real_part = jnp.einsum(pattern, tensor[0], shaped[0], precision=HIGHEST) - jnp.einsum(
        pattern, tensor[1], shaped[1], precision=HIGHEST
    )
    imag_part = jnp.einsum(pattern, tensor[1], shaped[0], precision=HIGHEST) + jnp.einsum(
        pattern, tensor[0], shaped[1], precision=HIGHEST
    )
    return jnp.stack([real_part, imag_part]).reshape(2, count_all)


def spare_sign(count_all, spare_values):
    lane_bits = 7
    spare_count = spare_values.shape[0]
    row_bits = spare_count - lane_bits
    lane_parity = jnp.sum(bit_table(lane_bits) * spare_values[None, :lane_bits], axis=1)
    row_parity = jnp.sum(bit_table(row_bits) * spare_values[None, lane_bits:], axis=1)
    repeat = count_all // (2**spare_count)
    parity = row_parity[:, None] + lane_parity[None, :]
    sign = (1 - 2 * (parity & 1)).astype(jnp.float32).reshape(1, 2**spare_count)
    return jnp.broadcast_to(sign, (repeat, 2**spare_count)).reshape(count_all)


def position_of(layout, wanted):
    places = jnp.arange(layout.shape[0], dtype=jnp.int32)
    return jnp.sum(jnp.where(layout[None, :] == wanted[:, None], places[None, :], 0), axis=1)


def arrange(layout, leading, trailing):
    layout_len = layout.shape[0]
    lead_count = leading.shape[0]
    trail_count = trailing.shape[0]
    in_lead = layout[:, None] == leading[None, :]
    in_trail = layout[:, None] == trailing[None, :]
    lead_any = jnp.any(in_lead, axis=1)
    trail_any = jnp.any(in_trail, axis=1)
    remaining = jnp.logical_not(jnp.logical_or(lead_any, trail_any)).astype(jnp.int32)
    lead_rank = jnp.sum(in_lead * jnp.arange(lead_count, dtype=jnp.int32)[None, :], axis=1)
    trail_rank = (
        layout_len
        - trail_count
        + jnp.sum(in_trail * jnp.arange(trail_count, dtype=jnp.int32)[None, :], axis=1)
    )
    target = jnp.where(
        lead_any,
        lead_rank,
        jnp.where(trail_any, trail_rank, lead_count + jnp.cumsum(remaining) - 1),
    )
    places = jnp.arange(layout_len, dtype=jnp.int32)
    lands = target[None, :] == places[:, None]
    source = jnp.sum(jnp.where(lands, places[None, :], 0), axis=1)
    new_layout = jnp.sum(jnp.where(lands, layout[None, :], 0), axis=1)
    return (new_layout, source)


def halves(values, place_bit):
    count_all = values.shape[1]
    shaped = values.reshape(2, count_all >> place_bit + 1, 2, 1 << place_bit)
    return (shaped[:, :, 0], shaped[:, :, 1])


def rejoin(lower_half, upper_half, received, own_bit):
    keep_lower = own_bit == 0
    new_lower = jnp.where(keep_lower, lower_half, received)
    new_upper = jnp.where(keep_lower, received, upper_half)
    return jnp.stack([new_lower, new_upper], axis=2).reshape(2, -1)


def trade_group(values, place_bit, bit_num):
    lower_half, upper_half = halves(values, place_bit)
    own_bit = jnp.right_shift(lax.axis_index("grp"), bit_num) & 1
    outgoing = jnp.where(own_bit == 0, upper_half, lower_half)
    received = swapped(outgoing, "grp", bit_num)
    return rejoin(lower_half, upper_half, received, own_bit)


def pair_exchange(values, place_bit, bit_num, matrix):
    length = values.shape[1]
    lane_bits = 7
    rows = length >> lane_bits
    row_bit = place_bit - lane_bits
    own_bit = jnp.right_shift(lax.axis_index("grp"), bit_num) & 1
    received = swapped(values, "grp", bit_num)
    place = jnp.arange(rows, dtype=jnp.int32)
    mask = 1 << row_bit
    agree = (place[:, None] | mask) == (place[None, :] | mask)
    pair_bit = jnp.right_shift(place, row_bit) & 1
    states = jnp.arange(4, dtype=jnp.int32)
    pick_out = ((own_bit + 2 * pair_bit)[:, None] == states[None, :]).astype(jnp.float32)
    pick_par = ((1 - own_bit + 2 * pair_bit)[:, None] == states[None, :]).astype(jnp.float32)
    blocks = []
    for pick_in in (pick_out, pick_par):
        for part in range(2):
            coef = jnp.dot(
                jnp.dot(pick_out, matrix[part], precision=HIGHEST), pick_in.T, precision=HIGHEST
            )
            blocks.append(jnp.where(agree, coef, 0.0))
    own_re, own_im, par_re, par_im = blocks
    operator = jnp.concatenate(
        [
            jnp.concatenate([own_re, -own_im, par_re, -par_im], axis=1),
            jnp.concatenate([own_im, own_re, par_im, par_re], axis=1),
        ],
        axis=0,
    )
    stacked = jnp.concatenate(
        [values.reshape(2 * rows, -1), received.reshape(2 * rows, -1)], axis=0
    )
    out = jnp.dot(operator, stacked, precision=HIGHEST, preferred_element_type=jnp.float32)
    return out.reshape(2, length)


def row_pair_operator(matrix, rows, pairs):
    place = jnp.arange(rows, dtype=jnp.int32)
    states = jnp.arange(4, dtype=jnp.int32)
    touched = 0
    real_part = None
    imag_part = None
    for bit_a, bit_c in pairs:
        touched = touched | 1 << bit_a | 1 << bit_c
        pair_state = (jnp.right_shift(place, bit_a) & 1) + 2 * (jnp.right_shift(place, bit_c) & 1)
        pick = (pair_state[:, None] == states[None, :]).astype(jnp.float32)
        factor_re = jnp.dot(jnp.dot(pick, matrix[0], precision=HIGHEST), pick.T, precision=HIGHEST)
        factor_im = jnp.dot(jnp.dot(pick, matrix[1], precision=HIGHEST), pick.T, precision=HIGHEST)
        if real_part is None:
            real_part, imag_part = factor_re, factor_im
        else:
            real_part, imag_part = (
                real_part * factor_re - imag_part * factor_im,
                real_part * factor_im + imag_part * factor_re,
            )
    agree = (place[:, None] | touched) == (place[None, :] | touched)
    real_part = jnp.where(agree, real_part, 0.0)
    imag_part = jnp.where(agree, imag_part, 0.0)
    return jnp.concatenate(
        [
            jnp.concatenate([real_part, -imag_part], axis=1),
            jnp.concatenate([imag_part, real_part], axis=1),
        ],
        axis=0,
    )


def field_exchange(values, field_bits):
    width = 2**field_bits
    own = lax.axis_index("grp") & width - 1
    shaped = values.reshape(2, -1, width, 2**7)
    received = {}
    for flip in range(1, width):
        outgoing = lax.dynamic_index_in_dim(shaped, own ^ flip, axis=2, keepdims=False)
        pairs = [(source, source ^ flip) for source in range(lax.axis_size("grp"))]
        received[flip] = lax.ppermute(outgoing, "grp", pairs)
    parts = []
    for place in range(width):
        chosen = shaped[:, :, place]
        for flip in range(1, width):
            chosen = jnp.where((own ^ place) == flip, received[flip], chosen)
        parts.append(chosen)
    return jnp.stack(parts, axis=2).reshape(values.shape)


def field_pair_gates(values, local_bits, field_bits, matrix):
    lane_bits = 7
    rows = values.shape[1] >> lane_bits
    pairs = [(bit_num, local_bits - 1 - bit_num - lane_bits) for bit_num in range(field_bits)]
    operator = row_pair_operator(matrix, rows, pairs)
    values = field_exchange(values, field_bits)
    values = jnp.dot(
        operator,
        values.reshape(2 * rows, -1),
        precision=HIGHEST,
        preferred_element_type=jnp.float32,
    ).reshape(values.shape)
    return field_exchange(values, field_bits)


def pair_operator(matrix, group_bits):
    size = 2 ** (2 * group_bits)
    place = jnp.arange(size, dtype=jnp.int32)
    states = jnp.arange(4, dtype=jnp.int32)
    real_part = None
    imag_part = None
    for bit_num in range(group_bits):
        pair_state = (jnp.right_shift(place, bit_num) & 1) + 2 * (
            jnp.right_shift(place, 2 * group_bits - 1 - bit_num) & 1
        )
        pick = (pair_state[:, None] == states[None, :]).astype(jnp.float32)
        factor_re = jnp.dot(
            jnp.dot(pick, matrix[0], precision=HIGHEST), pick.T, precision=HIGHEST
        )
        factor_im = jnp.dot(
            jnp.dot(pick, matrix[1], precision=HIGHEST), pick.T, precision=HIGHEST
        )
        if real_part is None:
            real_part, imag_part = factor_re, factor_im
        else:
            real_part, imag_part = (
                real_part * factor_re - imag_part * factor_im,
                real_part * factor_im + imag_part * factor_re,
            )
    return (real_part, imag_part)


def group_gates(values, local_bits, group_bits, matrix):
    length = values.shape[1]
    groups = 2**group_bits
    low = local_bits - 2 * group_bits
    shaped = values.reshape(2, groups, groups, 2**low)
    shaped = lax.all_to_all(shaped, "grp", split_axis=2, concat_axis=2, tiled=True)
    real_op, imag_op = pair_operator(matrix, group_bits)
    block = shaped.reshape(2, groups * groups, 2**low)
    real_part = jnp.dot(
        real_op, block[0], precision=HIGHEST, preferred_element_type=jnp.float32
    ) - jnp.dot(imag_op, block[1], precision=HIGHEST, preferred_element_type=jnp.float32)
    imag_part = jnp.dot(
        real_op, block[1], precision=HIGHEST, preferred_element_type=jnp.float32
    ) + jnp.dot(imag_op, block[0], precision=HIGHEST, preferred_element_type=jnp.float32)
    shaped = jnp.stack([real_part, imag_part]).reshape(2, groups, groups, 2**low)
    shaped = lax.all_to_all(shaped, "grp", split_axis=2, concat_axis=2, tiled=True)
    return shaped.reshape(2, length)


def per_device(
    amplitudes, joined_gates, pair_gate, layout_in, layout_out, gate_qubits, spare_values
):
    length = amplitudes.shape[-1]
    local_bits = length.bit_length() - 1
    devices = lax.axis_size("dev")
    device_bits = devices.bit_length() - 1
    groups = lax.axis_size("grp")
    group_bits = groups.bit_length() - 1
    span_size = joined_gates.shape[-1]
    values = amplitudes.reshape(2, length)
    nothing = jnp.zeros((0,), jnp.int32)
    layout = layout_in[:local_bits]
    for gate_num in range(2):
        layout, source = arrange(layout, gate_qubits[gate_num], nothing)
        values = complex_gate(
            reorder(values, source).reshape(2, -1, span_size), joined_gates[gate_num]
        ).reshape(2, length)
    leaving = layout_out[local_bits : local_bits + device_bits]
    layout, source = arrange(layout, nothing, leaving)
    values = reorder(values, source)
    shaped = values.reshape(2, devices, length // devices)
    values = lax.all_to_all(shaped, "dev", split_axis=1, concat_axis=1, tiled=True).reshape(
        2, length
    )
    layout = jnp.concatenate(
        [layout[: local_bits - device_bits], layout_in[local_bits : local_bits + device_bits]]
    )
    for gate_num in range(2, 4):
        layout, source = arrange(layout, gate_qubits[gate_num], nothing)
        values = complex_gate(
            reorder(values, source).reshape(2, -1, span_size), joined_gates[gate_num]
        ).reshape(2, length)
    values = reorder(values, position_of(layout, layout_out[:local_bits]))
    values = values * spare_sign(length, spare_values)
    field_bits = 2
    values = field_pair_gates(values, local_bits, field_bits, pair_gate)
    for bit_num in range(field_bits, group_bits):
        values = pair_exchange(values, local_bits - 1 - bit_num, bit_num, pair_gate)
    return values.reshape(amplitudes.shape)


def solution(mesh):
    in_specs = (P(None, "grp", "dev", None), P(), P(), P(), P(), P(), P())
    out_specs = P(None, "grp", "dev", None)
    return jax.shard_map(
        per_device, mesh=mesh, in_specs=in_specs, out_specs=out_specs, check_vma=False
    )
```

```python
import jax
import jax.numpy as jnp
from jax import lax
from jax.sharding import PartitionSpec as P

HIGHEST = lax.Precision.HIGHEST


def swapped(value, axis, bit):
    mask = 2**bit
    pairs = [(source, source ^ mask) for source in range(lax.axis_size(axis))]
    return lax.ppermute(value, axis, pairs)


def bit_table(bit_count):
    place = jnp.arange(2**bit_count, dtype=jnp.int32)[:, None]
    return jnp.right_shift(place, jnp.arange(bit_count, dtype=jnp.int32)[None, :]) & 1


def source_index(bit_order, bit_count):
    lane_bits = min(7, bit_count)
    lane_part = jnp.sum(
        jnp.left_shift(bit_table(lane_bits), bit_order[None, :lane_bits]), axis=1
    )
    row_part = jnp.sum(
        jnp.left_shift(bit_table(bit_count - lane_bits), bit_order[None, lane_bits:]), axis=1
    )
    return (row_part[:, None] + lane_part[None, :]).reshape(2**bit_count)


def reorder(values, source):
    bit_count = source.shape[0]
    length = 2**bit_count
    lane_bits = 7
    lanes = 2**lane_bits
    rows = length // lanes
    picked = source_index(source, bit_count)
    one_hot = (
        lax.broadcasted_iota(jnp.int32, (lanes, length), 0) == (picked & lanes - 1)[None, :]
    ).astype(jnp.float32)
    spread = jnp.dot(
        values.reshape(2 * rows, lanes),
        one_hot,
        precision=HIGHEST,
        preferred_element_type=jnp.float32,
    ).reshape(2, rows, length)
    row_hit = lax.broadcasted_iota(jnp.int32, (rows, length), 0) == jnp.right_shift(
        picked, lane_bits
    )[None, :]
    return jnp.sum(jnp.where(row_hit[None], spread, 0.0), axis=1)


def complex_gate(values, matrix):
    real_part = jnp.dot(
        values[0], matrix[0].T, precision=HIGHEST, preferred_element_type=jnp.float32
    ) - jnp.dot(values[1], matrix[1].T, precision=HIGHEST, preferred_element_type=jnp.float32)
    imag_part = jnp.dot(
        values[0], matrix[1].T, precision=HIGHEST, preferred_element_type=jnp.float32
    ) + jnp.dot(values[1], matrix[0].T, precision=HIGHEST, preferred_element_type=jnp.float32)
    return jnp.stack([real_part, imag_part])


def pair_apply(values, pos_a, pos_c, matrix):
    count_all = values.shape[1]
    lower_pos = min(pos_a, pos_c)
    upper_pos = max(pos_a, pos_c)
    shaped = values.reshape(
        2, count_all >> upper_pos + 1, 2, 1 << upper_pos - lower_pos - 1, 2, 1 << lower_pos
    )
    tensor = matrix.reshape(2, 2, 2, 2, 2)
    pattern = "uvwx,hwmxl->humvl"
    real_part = jnp.einsum(pattern, tensor[0], shaped[0], precision=HIGHEST) - jnp.einsum(
        pattern, tensor[1], shaped[1], precision=HIGHEST
    )
    imag_part = jnp.einsum(pattern, tensor[1], shaped[0], precision=HIGHEST) + jnp.einsum(
        pattern, tensor[0], shaped[1], precision=HIGHEST
    )
    return jnp.stack([real_part, imag_part]).reshape(2, count_all)


def spare_sign(count_all, spare_values):
    lane_bits = 7
    spare_count = spare_values.shape[0]
    row_bits = spare_count - lane_bits
    lane_parity = jnp.sum(bit_table(lane_bits) * spare_values[None, :lane_bits], axis=1)
    row_parity = jnp.sum(bit_table(row_bits) * spare_values[None, lane_bits:], axis=1)
    repeat = count_all // (2**spare_count)
    parity = row_parity[:, None] + lane_parity[None, :]
    sign = (1 - 2 * (parity & 1)).astype(jnp.float32).reshape(1, 2**spare_count)
    return jnp.broadcast_to(sign, (repeat, 2**spare_count)).reshape(count_all)


def position_of(layout, wanted):
    places = jnp.arange(layout.shape[0], dtype=jnp.int32)
    return jnp.sum(jnp.where(layout[None, :] == wanted[:, None], places[None, :], 0), axis=1)


def arrange(layout, leading, trailing):
    layout_len = layout.shape[0]
    lead_count = leading.shape[0]
    trail_count = trailing.shape[0]
    in_lead = layout[:, None] == leading[None, :]
    in_trail = layout[:, None] == trailing[None, :]
    lead_any = jnp.any(in_lead, axis=1)
    trail_any = jnp.any(in_trail, axis=1)
    remaining = jnp.logical_not(jnp.logical_or(lead_any, trail_any)).astype(jnp.int32)
    lead_rank = jnp.sum(in_lead * jnp.arange(lead_count, dtype=jnp.int32)[None, :], axis=1)
    trail_rank = (
        layout_len
        - trail_count
        + jnp.sum(in_trail * jnp.arange(trail_count, dtype=jnp.int32)[None, :], axis=1)
    )
    target = jnp.where(
        lead_any,
        lead_rank,
        jnp.where(trail_any, trail_rank, lead_count + jnp.cumsum(remaining) - 1),
    )
    places = jnp.arange(layout_len, dtype=jnp.int32)
    lands = target[None, :] == places[:, None]
    source = jnp.sum(jnp.where(lands, places[None, :], 0), axis=1)
    new_layout = jnp.sum(jnp.where(lands, layout[None, :], 0), axis=1)
    return (new_layout, source)


def halves(values, place_bit):
    count_all = values.shape[1]
    shaped = values.reshape(2, count_all >> place_bit + 1, 2, 1 << place_bit)
    return (shaped[:, :, 0], shaped[:, :, 1])


def rejoin(lower_half, upper_half, received, own_bit):
    keep_lower = own_bit == 0
    new_lower = jnp.where(keep_lower, lower_half, received)
    new_upper = jnp.where(keep_lower, received, upper_half)
    return jnp.stack([new_lower, new_upper], axis=2).reshape(2, -1)


def trade_group(values, place_bit, bit_num):
    lower_half, upper_half = halves(values, place_bit)
    own_bit = jnp.right_shift(lax.axis_index("grp"), bit_num) & 1
    outgoing = jnp.where(own_bit == 0, upper_half, lower_half)
    received = swapped(outgoing, "grp", bit_num)
    return rejoin(lower_half, upper_half, received, own_bit)


def pair_exchange(values, place_bit, bit_num, matrix):
    length = values.shape[1]
    lane_bits = 7
    rows = length >> lane_bits
    row_bit = place_bit - lane_bits
    own_bit = jnp.right_shift(lax.axis_index("grp"), bit_num) & 1
    received = swapped(values, "grp", bit_num)
    place = jnp.arange(rows, dtype=jnp.int32)
    mask = 1 << row_bit
    agree = (place[:, None] | mask) == (place[None, :] | mask)
    pair_bit = jnp.right_shift(place, row_bit) & 1
    states = jnp.arange(4, dtype=jnp.int32)
    pick_out = ((own_bit + 2 * pair_bit)[:, None] == states[None, :]).astype(jnp.float32)
    pick_par = ((1 - own_bit + 2 * pair_bit)[:, None] == states[None, :]).astype(jnp.float32)
    blocks = []
    for pick_in in (pick_out, pick_par):
        for part in range(2):
            coef = jnp.dot(
                jnp.dot(pick_out, matrix[part], precision=HIGHEST), pick_in.T, precision=HIGHEST
            )
            blocks.append(jnp.where(agree, coef, 0.0))
    own_re, own_im, par_re, par_im = blocks
    operator = jnp.concatenate(
        [
            jnp.concatenate([own_re, -own_im, par_re, -par_im], axis=1),
            jnp.concatenate([own_im, own_re, par_im, par_re], axis=1),
        ],
        axis=0,
    )
    stacked = jnp.concatenate(
        [values.reshape(2 * rows, -1), received.reshape(2 * rows, -1)], axis=0
    )
    out = jnp.dot(operator, stacked, precision=HIGHEST, preferred_element_type=jnp.float32)
    return out.reshape(2, length)


def gathered_pair_gates(values, local_bits, group_bits, matrix):
    length = values.shape[1]
    groups = 2**group_bits
    field = 2**group_bits
    rest = length // field
    own = lax.axis_index("grp")
    gathered = lax.all_gather(values, "grp", axis=0, tiled=False)
    block = gathered.reshape(groups, 2, field, rest).transpose(1, 0, 2, 3)
    block = block.reshape(2, groups * field, rest)
    out_place = jnp.arange(field, dtype=jnp.int32)
    in_place = jnp.arange(groups * field, dtype=jnp.int32)
    states = jnp.arange(4, dtype=jnp.int32)
    real_part = None
    imag_part = None
    for bit_num in range(group_bits):
        c_bit = group_bits - 1 - bit_num
        out_state = (jnp.right_shift(own, bit_num) & 1) + 2 * (
            jnp.right_shift(out_place, c_bit) & 1
        )
        in_state = (jnp.right_shift(in_place, group_bits + bit_num) & 1) + 2 * (
            jnp.right_shift(in_place, c_bit) & 1
        )
        pick_out = (out_state[:, None] == states[None, :]).astype(jnp.float32)
        pick_in = (in_state[:, None] == states[None, :]).astype(jnp.float32)
        factor_re = jnp.dot(jnp.dot(pick_out, matrix[0], precision=HIGHEST), pick_in.T, precision=HIGHEST)
        factor_im = jnp.dot(jnp.dot(pick_out, matrix[1], precision=HIGHEST), pick_in.T, precision=HIGHEST)
        if real_part is None:
            real_part, imag_part = factor_re, factor_im
        else:
            real_part, imag_part = (
                real_part * factor_re - imag_part * factor_im,
                real_part * factor_im + imag_part * factor_re,
            )
    operator = jnp.concatenate(
        [
            jnp.concatenate([real_part, -imag_part], axis=1),
            jnp.concatenate([imag_part, real_part], axis=1),
        ],
        axis=0,
    )
    out = jnp.dot(
        operator,
        block.reshape(2 * groups * field, rest),
        precision=HIGHEST,
        preferred_element_type=jnp.float32,
    )
    return out.reshape(2, length)


def pair_operator(matrix, group_bits):
    size = 2 ** (2 * group_bits)
    place = jnp.arange(size, dtype=jnp.int32)
    states = jnp.arange(4, dtype=jnp.int32)
    real_part = None
    imag_part = None
    for bit_num in range(group_bits):
        pair_state = (jnp.right_shift(place, bit_num) & 1) + 2 * (
            jnp.right_shift(place, 2 * group_bits - 1 - bit_num) & 1
        )
        pick = (pair_state[:, None] == states[None, :]).astype(jnp.float32)
        factor_re = jnp.dot(
            jnp.dot(pick, matrix[0], precision=HIGHEST), pick.T, precision=HIGHEST
        )
        factor_im = jnp.dot(
            jnp.dot(pick, matrix[1], precision=HIGHEST), pick.T, precision=HIGHEST
        )
        if real_part is None:
            real_part, imag_part = factor_re, factor_im
        else:
            real_part, imag_part = (
                real_part * factor_re - imag_part * factor_im,
                real_part * factor_im + imag_part * factor_re,
            )
    return (real_part, imag_part)


def group_gates(values, local_bits, group_bits, matrix):
    length = values.shape[1]
    groups = 2**group_bits
    low = local_bits - 2 * group_bits
    shaped = values.reshape(2, groups, groups, 2**low)
    shaped = lax.all_to_all(shaped, "grp", split_axis=2, concat_axis=2, tiled=True)
    real_op, imag_op = pair_operator(matrix, group_bits)
    block = shaped.reshape(2, groups * groups, 2**low)
    real_part = jnp.dot(
        real_op, block[0], precision=HIGHEST, preferred_element_type=jnp.float32
    ) - jnp.dot(imag_op, block[1], precision=HIGHEST, preferred_element_type=jnp.float32)
    imag_part = jnp.dot(
        real_op, block[1], precision=HIGHEST, preferred_element_type=jnp.float32
    ) + jnp.dot(imag_op, block[0], precision=HIGHEST, preferred_element_type=jnp.float32)
    shaped = jnp.stack([real_part, imag_part]).reshape(2, groups, groups, 2**low)
    shaped = lax.all_to_all(shaped, "grp", split_axis=2, concat_axis=2, tiled=True)
    return shaped.reshape(2, length)


def per_device(
    amplitudes, joined_gates, pair_gate, layout_in, layout_out, gate_qubits, spare_values
):
    length = amplitudes.shape[-1]
    local_bits = length.bit_length() - 1
    devices = lax.axis_size("dev")
    device_bits = devices.bit_length() - 1
    groups = lax.axis_size("grp")
    group_bits = groups.bit_length() - 1
    span_size = joined_gates.shape[-1]
    values = amplitudes.reshape(2, length)
    nothing = jnp.zeros((0,), jnp.int32)
    layout = layout_in[:local_bits]
    for gate_num in range(2):
        layout, source = arrange(layout, gate_qubits[gate_num], nothing)
        values = complex_gate(
            reorder(values, source).reshape(2, -1, span_size), joined_gates[gate_num]
        ).reshape(2, length)
    leaving = layout_out[local_bits : local_bits + device_bits]
    layout, source = arrange(layout, nothing, leaving)
    values = reorder(values, source)
    shaped = values.reshape(2, devices, length // devices)
    values = lax.all_to_all(shaped, "dev", split_axis=1, concat_axis=1, tiled=True).reshape(
        2, length
    )
    layout = jnp.concatenate(
        [layout[: local_bits - device_bits], layout_in[local_bits : local_bits + device_bits]]
    )
    for gate_num in range(2, 4):
        layout, source = arrange(layout, gate_qubits[gate_num], nothing)
        values = complex_gate(
            reorder(values, source).reshape(2, -1, span_size), joined_gates[gate_num]
        ).reshape(2, length)
    values = reorder(values, position_of(layout, layout_out[:local_bits]))
    values = values * spare_sign(length, spare_values)
    values = gathered_pair_gates(values, local_bits, group_bits, pair_gate)
    return values.reshape(amplitudes.shape)


def solution(mesh):
    in_specs = (P(None, "grp", "dev", None), P(), P(), P(), P(), P(), P())
    out_specs = P(None, "grp", "dev", None)
    return jax.shard_map(
        per_device, mesh=mesh, in_specs=in_specs, out_specs=out_specs, check_vma=False
    )
```

```python
import jax
import jax.numpy as jnp
from jax import lax
from jax.sharding import PartitionSpec as P

HIGHEST = lax.Precision.HIGHEST


def swapped(value, axis, bit):
    mask = 2**bit
    pairs = [(source, source ^ mask) for source in range(lax.axis_size(axis))]
    return lax.ppermute(value, axis, pairs)


def bit_table(bit_count):
    place = jnp.arange(2**bit_count, dtype=jnp.int32)[:, None]
    return jnp.right_shift(place, jnp.arange(bit_count, dtype=jnp.int32)[None, :]) & 1


def source_index(bit_order, bit_count):
    lane_bits = min(7, bit_count)
    lane_part = jnp.sum(
        jnp.left_shift(bit_table(lane_bits), bit_order[None, :lane_bits]), axis=1
    )
    row_part = jnp.sum(
        jnp.left_shift(bit_table(bit_count - lane_bits), bit_order[None, lane_bits:]), axis=1
    )
    return (row_part[:, None] + lane_part[None, :]).reshape(2**bit_count)


def reorder(values, source):
    bit_count = source.shape[0]
    length = 2**bit_count
    lane_bits = 7
    lanes = 2**lane_bits
    rows = length // lanes
    picked = source_index(source, bit_count)
    one_hot = (
        lax.broadcasted_iota(jnp.int32, (lanes, length), 0) == (picked & lanes - 1)[None, :]
    ).astype(jnp.float32)
    spread = jnp.dot(
        values.reshape(2 * rows, lanes),
        one_hot,
        precision=HIGHEST,
        preferred_element_type=jnp.float32,
    ).reshape(2, rows, length)
    row_hit = lax.broadcasted_iota(jnp.int32, (rows, length), 0) == jnp.right_shift(
        picked, lane_bits
    )[None, :]
    return jnp.sum(jnp.where(row_hit[None], spread, 0.0), axis=1)


def complex_gate(values, matrix):
    real_part = jnp.dot(
        values[0], matrix[0].T, precision=HIGHEST, preferred_element_type=jnp.float32
    ) - jnp.dot(values[1], matrix[1].T, precision=HIGHEST, preferred_element_type=jnp.float32)
    imag_part = jnp.dot(
        values[0], matrix[1].T, precision=HIGHEST, preferred_element_type=jnp.float32
    ) + jnp.dot(values[1], matrix[0].T, precision=HIGHEST, preferred_element_type=jnp.float32)
    return jnp.stack([real_part, imag_part])


def pair_apply(values, pos_a, pos_c, matrix):
    count_all = values.shape[1]
    lower_pos = min(pos_a, pos_c)
    upper_pos = max(pos_a, pos_c)
    shaped = values.reshape(
        2, count_all >> upper_pos + 1, 2, 1 << upper_pos - lower_pos - 1, 2, 1 << lower_pos
    )
    tensor = matrix.reshape(2, 2, 2, 2, 2)
    pattern = "uvwx,hwmxl->humvl"
    real_part = jnp.einsum(pattern, tensor[0], shaped[0], precision=HIGHEST) - jnp.einsum(
        pattern, tensor[1], shaped[1], precision=HIGHEST
    )
    imag_part = jnp.einsum(pattern, tensor[1], shaped[0], precision=HIGHEST) + jnp.einsum(
        pattern, tensor[0], shaped[1], precision=HIGHEST
    )
    return jnp.stack([real_part, imag_part]).reshape(2, count_all)


def spare_sign(count_all, spare_values):
    lane_bits = 7
    spare_count = spare_values.shape[0]
    row_bits = spare_count - lane_bits
    lane_parity = jnp.sum(bit_table(lane_bits) * spare_values[None, :lane_bits], axis=1)
    row_parity = jnp.sum(bit_table(row_bits) * spare_values[None, lane_bits:], axis=1)
    repeat = count_all // (2**spare_count)
    parity = row_parity[:, None] + lane_parity[None, :]
    sign = (1 - 2 * (parity & 1)).astype(jnp.float32).reshape(1, 2**spare_count)
    return jnp.broadcast_to(sign, (repeat, 2**spare_count)).reshape(count_all)


def position_of(layout, wanted):
    places = jnp.arange(layout.shape[0], dtype=jnp.int32)
    return jnp.sum(jnp.where(layout[None, :] == wanted[:, None], places[None, :], 0), axis=1)


def arrange(layout, leading, trailing):
    layout_len = layout.shape[0]
    lead_count = leading.shape[0]
    trail_count = trailing.shape[0]
    in_lead = layout[:, None] == leading[None, :]
    in_trail = layout[:, None] == trailing[None, :]
    lead_any = jnp.any(in_lead, axis=1)
    trail_any = jnp.any(in_trail, axis=1)
    remaining = jnp.logical_not(jnp.logical_or(lead_any, trail_any)).astype(jnp.int32)
    lead_rank = jnp.sum(in_lead * jnp.arange(lead_count, dtype=jnp.int32)[None, :], axis=1)
    trail_rank = (
        layout_len
        - trail_count
        + jnp.sum(in_trail * jnp.arange(trail_count, dtype=jnp.int32)[None, :], axis=1)
    )
    target = jnp.where(
        lead_any,
        lead_rank,
        jnp.where(trail_any, trail_rank, lead_count + jnp.cumsum(remaining) - 1),
    )
    places = jnp.arange(layout_len, dtype=jnp.int32)
    lands = target[None, :] == places[:, None]
    source = jnp.sum(jnp.where(lands, places[None, :], 0), axis=1)
    new_layout = jnp.sum(jnp.where(lands, layout[None, :], 0), axis=1)
    return (new_layout, source)


def halves(values, place_bit):
    count_all = values.shape[1]
    shaped = values.reshape(2, count_all >> place_bit + 1, 2, 1 << place_bit)
    return (shaped[:, :, 0], shaped[:, :, 1])


def rejoin(lower_half, upper_half, received, own_bit):
    keep_lower = own_bit == 0
    new_lower = jnp.where(keep_lower, lower_half, received)
    new_upper = jnp.where(keep_lower, received, upper_half)
    return jnp.stack([new_lower, new_upper], axis=2).reshape(2, -1)


def trade_group(values, place_bit, bit_num):
    lower_half, upper_half = halves(values, place_bit)
    own_bit = jnp.right_shift(lax.axis_index("grp"), bit_num) & 1
    outgoing = jnp.where(own_bit == 0, upper_half, lower_half)
    received = swapped(outgoing, "grp", bit_num)
    return rejoin(lower_half, upper_half, received, own_bit)


def pair_exchange(values, place_bit, bit_num, matrix):
    length = values.shape[1]
    lane_bits = 7
    rows = length >> lane_bits
    row_bit = place_bit - lane_bits
    own_bit = jnp.right_shift(lax.axis_index("grp"), bit_num) & 1
    received = swapped(values, "grp", bit_num)
    place = jnp.arange(rows, dtype=jnp.int32)
    mask = 1 << row_bit
    agree = (place[:, None] | mask) == (place[None, :] | mask)
    pair_bit = jnp.right_shift(place, row_bit) & 1
    states = jnp.arange(4, dtype=jnp.int32)
    pick_out = ((own_bit + 2 * pair_bit)[:, None] == states[None, :]).astype(jnp.float32)
    pick_par = ((1 - own_bit + 2 * pair_bit)[:, None] == states[None, :]).astype(jnp.float32)
    blocks = []
    for pick_in in (pick_out, pick_par):
        for part in range(2):
            coef = jnp.dot(
                jnp.dot(pick_out, matrix[part], precision=HIGHEST), pick_in.T, precision=HIGHEST
            )
            blocks.append(jnp.where(agree, coef, 0.0))
    own_re, own_im, par_re, par_im = blocks
    operator = jnp.concatenate(
        [
            jnp.concatenate([own_re, -own_im, par_re, -par_im], axis=1),
            jnp.concatenate([own_im, own_re, par_im, par_re], axis=1),
        ],
        axis=0,
    )
    stacked = jnp.concatenate(
        [values.reshape(2 * rows, -1), received.reshape(2 * rows, -1)], axis=0
    )
    out = jnp.dot(operator, stacked, precision=HIGHEST, preferred_element_type=jnp.float32)
    return out.reshape(2, length)


def pair_operator(matrix, group_bits):
    size = 2 ** (2 * group_bits)
    place = jnp.arange(size, dtype=jnp.int32)
    states = jnp.arange(4, dtype=jnp.int32)
    real_part = None
    imag_part = None
    for bit_num in range(group_bits):
        pair_state = (jnp.right_shift(place, bit_num) & 1) + 2 * (
            jnp.right_shift(place, 2 * group_bits - 1 - bit_num) & 1
        )
        pick = (pair_state[:, None] == states[None, :]).astype(jnp.float32)
        factor_re = jnp.dot(
            jnp.dot(pick, matrix[0], precision=HIGHEST), pick.T, precision=HIGHEST
        )
        factor_im = jnp.dot(
            jnp.dot(pick, matrix[1], precision=HIGHEST), pick.T, precision=HIGHEST
        )
        if real_part is None:
            real_part, imag_part = factor_re, factor_im
        else:
            real_part, imag_part = (
                real_part * factor_re - imag_part * factor_im,
                real_part * factor_im + imag_part * factor_re,
            )
    return (real_part, imag_part)


def group_gates(values, local_bits, group_bits, matrix):
    length = values.shape[1]
    groups = 2**group_bits
    low = local_bits - 2 * group_bits
    shaped = values.reshape(2, groups, groups, 2**low)
    shaped = lax.all_to_all(shaped, "grp", split_axis=2, concat_axis=2, tiled=True)
    real_op, imag_op = pair_operator(matrix, group_bits)
    block = shaped.reshape(2, groups * groups, 2**low)
    real_part = jnp.dot(
        real_op, block[0], precision=HIGHEST, preferred_element_type=jnp.float32
    ) - jnp.dot(imag_op, block[1], precision=HIGHEST, preferred_element_type=jnp.float32)
    imag_part = jnp.dot(
        real_op, block[1], precision=HIGHEST, preferred_element_type=jnp.float32
    ) + jnp.dot(imag_op, block[0], precision=HIGHEST, preferred_element_type=jnp.float32)
    shaped = jnp.stack([real_part, imag_part]).reshape(2, groups, groups, 2**low)
    shaped = lax.all_to_all(shaped, "grp", split_axis=2, concat_axis=2, tiled=True)
    return shaped.reshape(2, length)


def per_device(
    amplitudes, joined_gates, pair_gate, layout_in, layout_out, gate_qubits, spare_values
):
    length = amplitudes.shape[-1]
    local_bits = length.bit_length() - 1
    devices = lax.axis_size("dev")
    device_bits = devices.bit_length() - 1
    groups = lax.axis_size("grp")
    group_bits = groups.bit_length() - 1
    span_size = joined_gates.shape[-1]
    values = amplitudes.reshape(2, length)
    nothing = jnp.zeros((0,), jnp.int32)
    layout = layout_in[:local_bits]
    for gate_num in range(2):
        layout, source = arrange(layout, gate_qubits[gate_num], nothing)
        values = complex_gate(
            reorder(values, source).reshape(2, -1, span_size), joined_gates[gate_num]
        ).reshape(2, length)
    leaving = layout_out[local_bits : local_bits + device_bits]
    layout, source = arrange(layout, nothing, leaving)
    values = reorder(values, source)
    shaped = values.reshape(2, devices, length // devices)
    values = lax.all_to_all(shaped, "dev", split_axis=1, concat_axis=1, tiled=True).reshape(
        2, length
    )
    layout = jnp.concatenate(
        [layout[: local_bits - device_bits], layout_in[local_bits : local_bits + device_bits]]
    )
    for gate_num in range(2, 4):
        layout, source = arrange(layout, gate_qubits[gate_num], nothing)
        values = complex_gate(
            reorder(values, source).reshape(2, -1, span_size), joined_gates[gate_num]
        ).reshape(2, length)
    values = reorder(values, position_of(layout, layout_out[:local_bits]))
    values = values * spare_sign(length, spare_values)
    split_bit = 7
    shaped = values.reshape(2, length >> split_bit + 1, 2, 1 << split_bit)
    orders = (tuple(range(group_bits)), tuple(reversed(range(group_bits))))
    halves_out = []
    for half_num in range(2):
        half = shaped[:, :, half_num].reshape(2, length // 2)
        for bit_num in orders[half_num]:
            half = pair_exchange(half, local_bits - 2 - bit_num, bit_num, pair_gate)
        halves_out.append(half.reshape(2, length >> split_bit + 1, 1 << split_bit))
    values = jnp.stack(halves_out, axis=2).reshape(2, length)
    return values.reshape(amplitudes.shape)


def solution(mesh):
    in_specs = (P(None, "grp", "dev", None), P(), P(), P(), P(), P(), P())
    out_specs = P(None, "grp", "dev", None)
    return jax.shard_map(
        per_device, mesh=mesh, in_specs=in_specs, out_specs=out_specs, check_vma=False
    )
```

```python
import jax
import jax.numpy as jnp
from jax import lax
from jax.sharding import PartitionSpec as P

HIGHEST = lax.Precision.HIGHEST


def swapped(value, axis, bit):
    mask = 2**bit
    pairs = [(source, source ^ mask) for source in range(lax.axis_size(axis))]
    return lax.ppermute(value, axis, pairs)


def bit_table(bit_count):
    place = jnp.arange(2**bit_count, dtype=jnp.int32)[:, None]
    return jnp.right_shift(place, jnp.arange(bit_count, dtype=jnp.int32)[None, :]) & 1


def source_index(bit_order, bit_count):
    lane_bits = min(7, bit_count)
    lane_part = jnp.sum(
        jnp.left_shift(bit_table(lane_bits), bit_order[None, :lane_bits]), axis=1
    )
    row_part = jnp.sum(
        jnp.left_shift(bit_table(bit_count - lane_bits), bit_order[None, lane_bits:]), axis=1
    )
    return (row_part[:, None] + lane_part[None, :]).reshape(2**bit_count)


def reorder(values, source):
    bit_count = source.shape[0]
    length = 2**bit_count
    lane_bits = 8
    lanes = 2**lane_bits
    rows = length // lanes
    picked = source_index(source, bit_count)
    one_hot = (
        lax.broadcasted_iota(jnp.int32, (lanes, length), 0) == (picked & lanes - 1)[None, :]
    ).astype(jnp.float32)
    spread = jnp.dot(
        values.reshape(2 * rows, lanes),
        one_hot,
        precision=HIGHEST,
        preferred_element_type=jnp.float32,
    ).reshape(2, rows, length)
    row_hit = lax.broadcasted_iota(jnp.int32, (rows, length), 0) == jnp.right_shift(
        picked, lane_bits
    )[None, :]
    return jnp.sum(jnp.where(row_hit[None], spread, 0.0), axis=1)


def complex_gate(values, matrix):
    real_part = jnp.dot(
        values[0], matrix[0].T, precision=HIGHEST, preferred_element_type=jnp.float32
    ) - jnp.dot(values[1], matrix[1].T, precision=HIGHEST, preferred_element_type=jnp.float32)
    imag_part = jnp.dot(
        values[0], matrix[1].T, precision=HIGHEST, preferred_element_type=jnp.float32
    ) + jnp.dot(values[1], matrix[0].T, precision=HIGHEST, preferred_element_type=jnp.float32)
    return jnp.stack([real_part, imag_part])


def pair_apply(values, pos_a, pos_c, matrix):
    count_all = values.shape[1]
    lower_pos = min(pos_a, pos_c)
    upper_pos = max(pos_a, pos_c)
    shaped = values.reshape(
        2, count_all >> upper_pos + 1, 2, 1 << upper_pos - lower_pos - 1, 2, 1 << lower_pos
    )
    tensor = matrix.reshape(2, 2, 2, 2, 2)
    pattern = "uvwx,hwmxl->humvl"
    real_part = jnp.einsum(pattern, tensor[0], shaped[0], precision=HIGHEST) - jnp.einsum(
        pattern, tensor[1], shaped[1], precision=HIGHEST
    )
    imag_part = jnp.einsum(pattern, tensor[1], shaped[0], precision=HIGHEST) + jnp.einsum(
        pattern, tensor[0], shaped[1], precision=HIGHEST
    )
    return jnp.stack([real_part, imag_part]).reshape(2, count_all)


def spare_sign(count_all, spare_values):
    lane_bits = 7
    spare_count = spare_values.shape[0]
    row_bits = spare_count - lane_bits
    lane_parity = jnp.sum(bit_table(lane_bits) * spare_values[None, :lane_bits], axis=1)
    row_parity = jnp.sum(bit_table(row_bits) * spare_values[None, lane_bits:], axis=1)
    repeat = count_all // (2**spare_count)
    parity = row_parity[:, None] + lane_parity[None, :]
    sign = (1 - 2 * (parity & 1)).astype(jnp.float32).reshape(1, 2**spare_count)
    return jnp.broadcast_to(sign, (repeat, 2**spare_count)).reshape(count_all)


def position_of(layout, wanted):
    places = jnp.arange(layout.shape[0], dtype=jnp.int32)
    return jnp.sum(jnp.where(layout[None, :] == wanted[:, None], places[None, :], 0), axis=1)


def arrange(layout, leading, trailing):
    layout_len = layout.shape[0]
    lead_count = leading.shape[0]
    trail_count = trailing.shape[0]
    in_lead = layout[:, None] == leading[None, :]
    in_trail = layout[:, None] == trailing[None, :]
    lead_any = jnp.any(in_lead, axis=1)
    trail_any = jnp.any(in_trail, axis=1)
    remaining = jnp.logical_not(jnp.logical_or(lead_any, trail_any)).astype(jnp.int32)
    lead_rank = jnp.sum(in_lead * jnp.arange(lead_count, dtype=jnp.int32)[None, :], axis=1)
    trail_rank = (
        layout_len
        - trail_count
        + jnp.sum(in_trail * jnp.arange(trail_count, dtype=jnp.int32)[None, :], axis=1)
    )
    target = jnp.where(
        lead_any,
        lead_rank,
        jnp.where(trail_any, trail_rank, lead_count + jnp.cumsum(remaining) - 1),
    )
    places = jnp.arange(layout_len, dtype=jnp.int32)
    lands = target[None, :] == places[:, None]
    source = jnp.sum(jnp.where(lands, places[None, :], 0), axis=1)
    new_layout = jnp.sum(jnp.where(lands, layout[None, :], 0), axis=1)
    return (new_layout, source)


def halves(values, place_bit):
    count_all = values.shape[1]
    shaped = values.reshape(2, count_all >> place_bit + 1, 2, 1 << place_bit)
    return (shaped[:, :, 0], shaped[:, :, 1])


def rejoin(lower_half, upper_half, received, own_bit):
    keep_lower = own_bit == 0
    new_lower = jnp.where(keep_lower, lower_half, received)
    new_upper = jnp.where(keep_lower, received, upper_half)
    return jnp.stack([new_lower, new_upper], axis=2).reshape(2, -1)


def trade_group(values, place_bit, bit_num):
    lower_half, upper_half = halves(values, place_bit)
    own_bit = jnp.right_shift(lax.axis_index("grp"), bit_num) & 1
    outgoing = jnp.where(own_bit == 0, upper_half, lower_half)
    received = swapped(outgoing, "grp", bit_num)
    return rejoin(lower_half, upper_half, received, own_bit)


def pair_exchange(values, place_bit, bit_num, matrix):
    length = values.shape[1]
    lane_bits = 7
    rows = length >> lane_bits
    row_bit = place_bit - lane_bits
    own_bit = jnp.right_shift(lax.axis_index("grp"), bit_num) & 1
    received = swapped(values, "grp", bit_num)
    place = jnp.arange(rows, dtype=jnp.int32)
    mask = 1 << row_bit
    agree = (place[:, None] | mask) == (place[None, :] | mask)
    pair_bit = jnp.right_shift(place, row_bit) & 1
    states = jnp.arange(4, dtype=jnp.int32)
    pick_out = ((own_bit + 2 * pair_bit)[:, None] == states[None, :]).astype(jnp.float32)
    pick_par = ((1 - own_bit + 2 * pair_bit)[:, None] == states[None, :]).astype(jnp.float32)
    blocks = []
    for pick_in in (pick_out, pick_par):
        for part in range(2):
            coef = jnp.dot(
                jnp.dot(pick_out, matrix[part], precision=HIGHEST), pick_in.T, precision=HIGHEST
            )
            blocks.append(jnp.where(agree, coef, 0.0))
    own_re, own_im, par_re, par_im = blocks
    operator = jnp.concatenate(
        [
            jnp.concatenate([own_re, -own_im, par_re, -par_im], axis=1),
            jnp.concatenate([own_im, own_re, par_im, par_re], axis=1),
        ],
        axis=0,
    )
    stacked = jnp.concatenate(
        [values.reshape(2 * rows, -1), received.reshape(2 * rows, -1)], axis=0
    )
    out = jnp.dot(operator, stacked, precision=HIGHEST, preferred_element_type=jnp.float32)
    return out.reshape(2, length)


def pair_operator(matrix, group_bits):
    size = 2 ** (2 * group_bits)
    place = jnp.arange(size, dtype=jnp.int32)
    states = jnp.arange(4, dtype=jnp.int32)
    real_part = None
    imag_part = None
    for bit_num in range(group_bits):
        pair_state = (jnp.right_shift(place, bit_num) & 1) + 2 * (
            jnp.right_shift(place, 2 * group_bits - 1 - bit_num) & 1
        )
        pick = (pair_state[:, None] == states[None, :]).astype(jnp.float32)
        factor_re = jnp.dot(
            jnp.dot(pick, matrix[0], precision=HIGHEST), pick.T, precision=HIGHEST
        )
        factor_im = jnp.dot(
            jnp.dot(pick, matrix[1], precision=HIGHEST), pick.T, precision=HIGHEST
        )
        if real_part is None:
            real_part, imag_part = factor_re, factor_im
        else:
            real_part, imag_part = (
                real_part * factor_re - imag_part * factor_im,
                real_part * factor_im + imag_part * factor_re,
            )
    return (real_part, imag_part)


def group_gates(values, local_bits, group_bits, matrix):
    length = values.shape[1]
    groups = 2**group_bits
    low = local_bits - 2 * group_bits
    shaped = values.reshape(2, groups, groups, 2**low)
    shaped = lax.all_to_all(shaped, "grp", split_axis=2, concat_axis=2, tiled=True)
    real_op, imag_op = pair_operator(matrix, group_bits)
    block = shaped.reshape(2, groups * groups, 2**low)
    real_part = jnp.dot(
        real_op, block[0], precision=HIGHEST, preferred_element_type=jnp.float32
    ) - jnp.dot(imag_op, block[1], precision=HIGHEST, preferred_element_type=jnp.float32)
    imag_part = jnp.dot(
        real_op, block[1], precision=HIGHEST, preferred_element_type=jnp.float32
    ) + jnp.dot(imag_op, block[0], precision=HIGHEST, preferred_element_type=jnp.float32)
    shaped = jnp.stack([real_part, imag_part]).reshape(2, groups, groups, 2**low)
    shaped = lax.all_to_all(shaped, "grp", split_axis=2, concat_axis=2, tiled=True)
    return shaped.reshape(2, length)


def per_device(
    amplitudes, joined_gates, pair_gate, layout_in, layout_out, gate_qubits, spare_values
):
    length = amplitudes.shape[-1]
    local_bits = length.bit_length() - 1
    devices = lax.axis_size("dev")
    device_bits = devices.bit_length() - 1
    groups = lax.axis_size("grp")
    group_bits = groups.bit_length() - 1
    span_size = joined_gates.shape[-1]
    values = amplitudes.reshape(2, length)
    nothing = jnp.zeros((0,), jnp.int32)
    layout = layout_in[:local_bits]
    for gate_num in range(2):
        layout, source = arrange(layout, gate_qubits[gate_num], nothing)
        values = complex_gate(
            reorder(values, source).reshape(2, -1, span_size), joined_gates[gate_num]
        ).reshape(2, length)
    leaving = layout_out[local_bits : local_bits + device_bits]
    layout, source = arrange(layout, nothing, leaving)
    values = reorder(values, source)
    shaped = values.reshape(2, devices, length // devices)
    values = lax.all_to_all(shaped, "dev", split_axis=1, concat_axis=1, tiled=True).reshape(
        2, length
    )
    layout = jnp.concatenate(
        [layout[: local_bits - device_bits], layout_in[local_bits : local_bits + device_bits]]
    )
    for gate_num in range(2, 4):
        layout, source = arrange(layout, gate_qubits[gate_num], nothing)
        values = complex_gate(
            reorder(values, source).reshape(2, -1, span_size), joined_gates[gate_num]
        ).reshape(2, length)
    values = reorder(values, position_of(layout, layout_out[:local_bits]))
    values = values * spare_sign(length, spare_values)
    for bit_num in range(group_bits):
        values = pair_exchange(values, local_bits - 1 - bit_num, bit_num, pair_gate)
    return values.reshape(amplitudes.shape)


def solution(mesh):
    in_specs = (P(None, "grp", "dev", None), P(), P(), P(), P(), P(), P())
    out_specs = P(None, "grp", "dev", None)
    return jax.shard_map(
        per_device, mesh=mesh, in_specs=in_specs, out_specs=out_specs, check_vma=False
    )
```

```python
import jax
import jax.numpy as jnp
from jax import lax
from jax.sharding import PartitionSpec as P

HIGHEST = lax.Precision.HIGHEST


def swapped(value, axis, bit):
    mask = 2**bit
    pairs = [(source, source ^ mask) for source in range(lax.axis_size(axis))]
    return lax.ppermute(value, axis, pairs)


def bit_table(bit_count):
    place = jnp.arange(2**bit_count, dtype=jnp.int32)[:, None]
    return jnp.right_shift(place, jnp.arange(bit_count, dtype=jnp.int32)[None, :]) & 1


def source_index(bit_order, bit_count):
    lane_bits = min(7, bit_count)
    lane_part = jnp.sum(
        jnp.left_shift(bit_table(lane_bits), bit_order[None, :lane_bits]), axis=1
    )
    row_part = jnp.sum(
        jnp.left_shift(bit_table(bit_count - lane_bits), bit_order[None, lane_bits:]), axis=1
    )
    return (row_part[:, None] + lane_part[None, :]).reshape(2**bit_count)


def reorder(values, source):
    bit_count = source.shape[0]
    length = 2**bit_count
    lane_bits = 6
    lanes = 2**lane_bits
    rows = length // lanes
    picked = source_index(source, bit_count)
    one_hot = (
        lax.broadcasted_iota(jnp.int32, (lanes, length), 0) == (picked & lanes - 1)[None, :]
    ).astype(jnp.float32)
    spread = jnp.dot(
        values.reshape(2 * rows, lanes),
        one_hot,
        precision=HIGHEST,
        preferred_element_type=jnp.float32,
    ).reshape(2, rows, length)
    row_hit = lax.broadcasted_iota(jnp.int32, (rows, length), 0) == jnp.right_shift(
        picked, lane_bits
    )[None, :]
    return jnp.sum(jnp.where(row_hit[None], spread, 0.0), axis=1)


def complex_gate(values, matrix):
    real_part = jnp.dot(
        values[0], matrix[0].T, precision=HIGHEST, preferred_element_type=jnp.float32
    ) - jnp.dot(values[1], matrix[1].T, precision=HIGHEST, preferred_element_type=jnp.float32)
    imag_part = jnp.dot(
        values[0], matrix[1].T, precision=HIGHEST, preferred_element_type=jnp.float32
    ) + jnp.dot(values[1], matrix[0].T, precision=HIGHEST, preferred_element_type=jnp.float32)
    return jnp.stack([real_part, imag_part])


def pair_apply(values, pos_a, pos_c, matrix):
    count_all = values.shape[1]
    lower_pos = min(pos_a, pos_c)
    upper_pos = max(pos_a, pos_c)
    shaped = values.reshape(
        2, count_all >> upper_pos + 1, 2, 1 << upper_pos - lower_pos - 1, 2, 1 << lower_pos
    )
    tensor = matrix.reshape(2, 2, 2, 2, 2)
    pattern = "uvwx,hwmxl->humvl"
    real_part = jnp.einsum(pattern, tensor[0], shaped[0], precision=HIGHEST) - jnp.einsum(
        pattern, tensor[1], shaped[1], precision=HIGHEST
    )
    imag_part = jnp.einsum(pattern, tensor[1], shaped[0], precision=HIGHEST) + jnp.einsum(
        pattern, tensor[0], shaped[1], precision=HIGHEST
    )
    return jnp.stack([real_part, imag_part]).reshape(2, count_all)


def spare_sign(count_all, spare_values):
    lane_bits = 7
    spare_count = spare_values.shape[0]
    row_bits = spare_count - lane_bits
    lane_parity = jnp.sum(bit_table(lane_bits) * spare_values[None, :lane_bits], axis=1)
    row_parity = jnp.sum(bit_table(row_bits) * spare_values[None, lane_bits:], axis=1)
    repeat = count_all // (2**spare_count)
    parity = row_parity[:, None] + lane_parity[None, :]
    sign = (1 - 2 * (parity & 1)).astype(jnp.float32).reshape(1, 2**spare_count)
    return jnp.broadcast_to(sign, (repeat, 2**spare_count)).reshape(count_all)


def position_of(layout, wanted):
    places = jnp.arange(layout.shape[0], dtype=jnp.int32)
    return jnp.sum(jnp.where(layout[None, :] == wanted[:, None], places[None, :], 0), axis=1)


def arrange(layout, leading, trailing):
    layout_len = layout.shape[0]
    lead_count = leading.shape[0]
    trail_count = trailing.shape[0]
    in_lead = layout[:, None] == leading[None, :]
    in_trail = layout[:, None] == trailing[None, :]
    lead_any = jnp.any(in_lead, axis=1)
    trail_any = jnp.any(in_trail, axis=1)
    remaining = jnp.logical_not(jnp.logical_or(lead_any, trail_any)).astype(jnp.int32)
    lead_rank = jnp.sum(in_lead * jnp.arange(lead_count, dtype=jnp.int32)[None, :], axis=1)
    trail_rank = (
        layout_len
        - trail_count
        + jnp.sum(in_trail * jnp.arange(trail_count, dtype=jnp.int32)[None, :], axis=1)
    )
    target = jnp.where(
        lead_any,
        lead_rank,
        jnp.where(trail_any, trail_rank, lead_count + jnp.cumsum(remaining) - 1),
    )
    places = jnp.arange(layout_len, dtype=jnp.int32)
    lands = target[None, :] == places[:, None]
    source = jnp.sum(jnp.where(lands, places[None, :], 0), axis=1)
    new_layout = jnp.sum(jnp.where(lands, layout[None, :], 0), axis=1)
    return (new_layout, source)


def halves(values, place_bit):
    count_all = values.shape[1]
    shaped = values.reshape(2, count_all >> place_bit + 1, 2, 1 << place_bit)
    return (shaped[:, :, 0], shaped[:, :, 1])


def rejoin(lower_half, upper_half, received, own_bit):
    keep_lower = own_bit == 0
    new_lower = jnp.where(keep_lower, lower_half, received)
    new_upper = jnp.where(keep_lower, received, upper_half)
    return jnp.stack([new_lower, new_upper], axis=2).reshape(2, -1)


def trade_group(values, place_bit, bit_num):
    lower_half, upper_half = halves(values, place_bit)
    own_bit = jnp.right_shift(lax.axis_index("grp"), bit_num) & 1
    outgoing = jnp.where(own_bit == 0, upper_half, lower_half)
    received = swapped(outgoing, "grp", bit_num)
    return rejoin(lower_half, upper_half, received, own_bit)


def pair_exchange(values, place_bit, bit_num, matrix):
    length = values.shape[1]
    lane_bits = 7
    rows = length >> lane_bits
    row_bit = place_bit - lane_bits
    own_bit = jnp.right_shift(lax.axis_index("grp"), bit_num) & 1
    received = swapped(values, "grp", bit_num)
    place = jnp.arange(rows, dtype=jnp.int32)
    mask = 1 << row_bit
    agree = (place[:, None] | mask) == (place[None, :] | mask)
    pair_bit = jnp.right_shift(place, row_bit) & 1
    states = jnp.arange(4, dtype=jnp.int32)
    pick_out = ((own_bit + 2 * pair_bit)[:, None] == states[None, :]).astype(jnp.float32)
    pick_par = ((1 - own_bit + 2 * pair_bit)[:, None] == states[None, :]).astype(jnp.float32)
    blocks = []
    for pick_in in (pick_out, pick_par):
        for part in range(2):
            coef = jnp.dot(
                jnp.dot(pick_out, matrix[part], precision=HIGHEST), pick_in.T, precision=HIGHEST
            )
            blocks.append(jnp.where(agree, coef, 0.0))
    own_re, own_im, par_re, par_im = blocks
    operator = jnp.concatenate(
        [
            jnp.concatenate([own_re, -own_im, par_re, -par_im], axis=1),
            jnp.concatenate([own_im, own_re, par_im, par_re], axis=1),
        ],
        axis=0,
    )
    stacked = jnp.concatenate(
        [values.reshape(2 * rows, -1), received.reshape(2 * rows, -1)], axis=0
    )
    out = jnp.dot(operator, stacked, precision=HIGHEST, preferred_element_type=jnp.float32)
    return out.reshape(2, length)


def pair_operator(matrix, group_bits):
    size = 2 ** (2 * group_bits)
    place = jnp.arange(size, dtype=jnp.int32)
    states = jnp.arange(4, dtype=jnp.int32)
    real_part = None
    imag_part = None
    for bit_num in range(group_bits):
        pair_state = (jnp.right_shift(place, bit_num) & 1) + 2 * (
            jnp.right_shift(place, 2 * group_bits - 1 - bit_num) & 1
        )
        pick = (pair_state[:, None] == states[None, :]).astype(jnp.float32)
        factor_re = jnp.dot(
            jnp.dot(pick, matrix[0], precision=HIGHEST), pick.T, precision=HIGHEST
        )
        factor_im = jnp.dot(
            jnp.dot(pick, matrix[1], precision=HIGHEST), pick.T, precision=HIGHEST
        )
        if real_part is None:
            real_part, imag_part = factor_re, factor_im
        else:
            real_part, imag_part = (
                real_part * factor_re - imag_part * factor_im,
                real_part * factor_im + imag_part * factor_re,
            )
    return (real_part, imag_part)


def group_gates(values, local_bits, group_bits, matrix):
    length = values.shape[1]
    groups = 2**group_bits
    low = local_bits - 2 * group_bits
    shaped = values.reshape(2, groups, groups, 2**low)
    shaped = lax.all_to_all(shaped, "grp", split_axis=2, concat_axis=2, tiled=True)
    real_op, imag_op = pair_operator(matrix, group_bits)
    block = shaped.reshape(2, groups * groups, 2**low)
    real_part = jnp.dot(
        real_op, block[0], precision=HIGHEST, preferred_element_type=jnp.float32
    ) - jnp.dot(imag_op, block[1], precision=HIGHEST, preferred_element_type=jnp.float32)
    imag_part = jnp.dot(
        real_op, block[1], precision=HIGHEST, preferred_element_type=jnp.float32
    ) + jnp.dot(imag_op, block[0], precision=HIGHEST, preferred_element_type=jnp.float32)
    shaped = jnp.stack([real_part, imag_part]).reshape(2, groups, groups, 2**low)
    shaped = lax.all_to_all(shaped, "grp", split_axis=2, concat_axis=2, tiled=True)
    return shaped.reshape(2, length)


def per_device(
    amplitudes, joined_gates, pair_gate, layout_in, layout_out, gate_qubits, spare_values
):
    length = amplitudes.shape[-1]
    local_bits = length.bit_length() - 1
    devices = lax.axis_size("dev")
    device_bits = devices.bit_length() - 1
    groups = lax.axis_size("grp")
    group_bits = groups.bit_length() - 1
    span_size = joined_gates.shape[-1]
    values = amplitudes.reshape(2, length)
    nothing = jnp.zeros((0,), jnp.int32)
    layout = layout_in[:local_bits]
    for gate_num in range(2):
        layout, source = arrange(layout, gate_qubits[gate_num], nothing)
        values = complex_gate(
            reorder(values, source).reshape(2, -1, span_size), joined_gates[gate_num]
        ).reshape(2, length)
    leaving = layout_out[local_bits : local_bits + device_bits]
    layout, source = arrange(layout, nothing, leaving)
    values = reorder(values, source)
    shaped = values.reshape(2, devices, length // devices)
    values = lax.all_to_all(shaped, "dev", split_axis=1, concat_axis=1, tiled=True).reshape(
        2, length
    )
    layout = jnp.concatenate(
        [layout[: local_bits - device_bits], layout_in[local_bits : local_bits + device_bits]]
    )
    for gate_num in range(2, 4):
        layout, source = arrange(layout, gate_qubits[gate_num], nothing)
        values = complex_gate(
            reorder(values, source).reshape(2, -1, span_size), joined_gates[gate_num]
        ).reshape(2, length)
    values = reorder(values, position_of(layout, layout_out[:local_bits]))
    values = values * spare_sign(length, spare_values)
    for bit_num in range(group_bits):
        values = pair_exchange(values, local_bits - 1 - bit_num, bit_num, pair_gate)
    return values.reshape(amplitudes.shape)


def solution(mesh):
    in_specs = (P(None, "grp", "dev", None), P(), P(), P(), P(), P(), P())
    out_specs = P(None, "grp", "dev", None)
    return jax.shard_map(
        per_device, mesh=mesh, in_specs=in_specs, out_specs=out_specs, check_vma=False
    )
```

```python
import jax
import jax.numpy as jnp
from jax import lax
from jax.sharding import PartitionSpec as P

HIGHEST = lax.Precision.HIGHEST


def swapped(value, axis, bit):
    mask = 2**bit
    pairs = [(source, source ^ mask) for source in range(lax.axis_size(axis))]
    return lax.ppermute(value, axis, pairs)


def bit_table(bit_count):
    place = jnp.arange(2**bit_count, dtype=jnp.int32)[:, None]
    return jnp.right_shift(place, jnp.arange(bit_count, dtype=jnp.int32)[None, :]) & 1


def source_index(bit_order, bit_count):
    lane_bits = min(7, bit_count)
    lane_part = jnp.sum(
        jnp.left_shift(bit_table(lane_bits), bit_order[None, :lane_bits]), axis=1
    )
    row_part = jnp.sum(
        jnp.left_shift(bit_table(bit_count - lane_bits), bit_order[None, lane_bits:]), axis=1
    )
    return (row_part[:, None] + lane_part[None, :]).reshape(2**bit_count)


def reorder(values, source):
    bit_count = source.shape[0]
    length = 2**bit_count
    lane_bits = 7
    lanes = 2**lane_bits
    rows = length // lanes
    picked = source_index(source, bit_count)
    one_hot = (
        lax.broadcasted_iota(jnp.int32, (lanes, length), 0) == (picked & lanes - 1)[None, :]
    ).astype(jnp.float32)
    spread = jnp.dot(
        values.reshape(2 * rows, lanes),
        one_hot,
        precision=HIGHEST,
        preferred_element_type=jnp.float32,
    ).reshape(2, rows, length)
    row_hit = lax.broadcasted_iota(jnp.int32, (rows, length), 0) == jnp.right_shift(
        picked, lane_bits
    )[None, :]
    return jnp.sum(jnp.where(row_hit[None], spread, 0.0), axis=1)


def complex_gate(values, matrix):
    real_part = jnp.dot(
        values[0], matrix[0].T, precision=HIGHEST, preferred_element_type=jnp.float32
    ) - jnp.dot(values[1], matrix[1].T, precision=HIGHEST, preferred_element_type=jnp.float32)
    imag_part = jnp.dot(
        values[0], matrix[1].T, precision=HIGHEST, preferred_element_type=jnp.float32
    ) + jnp.dot(values[1], matrix[0].T, precision=HIGHEST, preferred_element_type=jnp.float32)
    return jnp.stack([real_part, imag_part])


def pair_apply(values, pos_a, pos_c, matrix):
    count_all = values.shape[1]
    lower_pos = min(pos_a, pos_c)
    upper_pos = max(pos_a, pos_c)
    shaped = values.reshape(
        2, count_all >> upper_pos + 1, 2, 1 << upper_pos - lower_pos - 1, 2, 1 << lower_pos
    )
    tensor = matrix.reshape(2, 2, 2, 2, 2)
    pattern = "uvwx,hwmxl->humvl"
    real_part = jnp.einsum(pattern, tensor[0], shaped[0], precision=HIGHEST) - jnp.einsum(
        pattern, tensor[1], shaped[1], precision=HIGHEST
    )
    imag_part = jnp.einsum(pattern, tensor[1], shaped[0], precision=HIGHEST) + jnp.einsum(
        pattern, tensor[0], shaped[1], precision=HIGHEST
    )
    return jnp.stack([real_part, imag_part]).reshape(2, count_all)


def spare_sign(count_all, spare_values):
    lane_bits = 7
    spare_count = spare_values.shape[0]
    row_bits = spare_count - lane_bits
    lane_parity = jnp.sum(bit_table(lane_bits) * spare_values[None, :lane_bits], axis=1)
    row_parity = jnp.sum(bit_table(row_bits) * spare_values[None, lane_bits:], axis=1)
    repeat = count_all // (2**spare_count)
    parity = row_parity[:, None] + lane_parity[None, :]
    sign = (1 - 2 * (parity & 1)).astype(jnp.float32).reshape(1, 2**spare_count)
    return jnp.broadcast_to(sign, (repeat, 2**spare_count)).reshape(count_all)


def position_of(layout, wanted):
    places = jnp.arange(layout.shape[0], dtype=jnp.int32)
    return jnp.sum(jnp.where(layout[None, :] == wanted[:, None], places[None, :], 0), axis=1)


def arrange(layout, leading, trailing):
    layout_len = layout.shape[0]
    lead_count = leading.shape[0]
    trail_count = trailing.shape[0]
    in_lead = layout[:, None] == leading[None, :]
    in_trail = layout[:, None] == trailing[None, :]
    lead_any = jnp.any(in_lead, axis=1)
    trail_any = jnp.any(in_trail, axis=1)
    remaining = jnp.logical_not(jnp.logical_or(lead_any, trail_any)).astype(jnp.int32)
    lead_rank = jnp.sum(in_lead * jnp.arange(lead_count, dtype=jnp.int32)[None, :], axis=1)
    trail_rank = (
        layout_len
        - trail_count
        + jnp.sum(in_trail * jnp.arange(trail_count, dtype=jnp.int32)[None, :], axis=1)
    )
    target = jnp.where(
        lead_any,
        lead_rank,
        jnp.where(trail_any, trail_rank, lead_count + jnp.cumsum(remaining) - 1),
    )
    places = jnp.arange(layout_len, dtype=jnp.int32)
    lands = target[None, :] == places[:, None]
    source = jnp.sum(jnp.where(lands, places[None, :], 0), axis=1)
    new_layout = jnp.sum(jnp.where(lands, layout[None, :], 0), axis=1)
    return (new_layout, source)


def halves(values, place_bit):
    count_all = values.shape[1]
    shaped = values.reshape(2, count_all >> place_bit + 1, 2, 1 << place_bit)
    return (shaped[:, :, 0], shaped[:, :, 1])


def rejoin(lower_half, upper_half, received, own_bit):
    keep_lower = own_bit == 0
    new_lower = jnp.where(keep_lower, lower_half, received)
    new_upper = jnp.where(keep_lower, received, upper_half)
    return jnp.stack([new_lower, new_upper], axis=2).reshape(2, -1)


def trade_group(values, place_bit, bit_num):
    lower_half, upper_half = halves(values, place_bit)
    own_bit = jnp.right_shift(lax.axis_index("grp"), bit_num) & 1
    outgoing = jnp.where(own_bit == 0, upper_half, lower_half)
    received = swapped(outgoing, "grp", bit_num)
    return rejoin(lower_half, upper_half, received, own_bit)


def pair_exchange(values, place_bit, bit_num, matrix):
    length = values.shape[1]
    lane_bits = 7
    rows = length >> lane_bits
    row_bit = place_bit - lane_bits
    own_bit = jnp.right_shift(lax.axis_index("grp"), bit_num) & 1
    received = swapped(values, "grp", bit_num)
    place = jnp.arange(rows, dtype=jnp.int32)
    mask = 1 << row_bit
    agree = (place[:, None] | mask) == (place[None, :] | mask)
    pair_bit = jnp.right_shift(place, row_bit) & 1
    states = jnp.arange(4, dtype=jnp.int32)
    pick_out = ((own_bit + 2 * pair_bit)[:, None] == states[None, :]).astype(jnp.float32)
    pick_par = ((1 - own_bit + 2 * pair_bit)[:, None] == states[None, :]).astype(jnp.float32)
    blocks = []
    for pick_in in (pick_out, pick_par):
        for part in range(2):
            coef = jnp.dot(
                jnp.dot(pick_out, matrix[part], precision=HIGHEST), pick_in.T, precision=HIGHEST
            )
            blocks.append(jnp.where(agree, coef, 0.0))
    own_re, own_im, par_re, par_im = blocks
    operator = jnp.concatenate(
        [
            jnp.concatenate([own_re, -own_im, par_re, -par_im], axis=1),
            jnp.concatenate([own_im, own_re, par_im, par_re], axis=1),
        ],
        axis=0,
    )
    stacked = jnp.concatenate(
        [values.reshape(2 * rows, -1), received.reshape(2 * rows, -1)], axis=0
    )
    out = jnp.dot(operator, stacked, precision=HIGHEST, preferred_element_type=jnp.float32)
    return out.reshape(2, length)


def pair_operator(matrix, group_bits):
    size = 2 ** (2 * group_bits)
    place = jnp.arange(size, dtype=jnp.int32)
    states = jnp.arange(4, dtype=jnp.int32)
    real_part = None
    imag_part = None
    for bit_num in range(group_bits):
        pair_state = (jnp.right_shift(place, bit_num) & 1) + 2 * (
            jnp.right_shift(place, 2 * group_bits - 1 - bit_num) & 1
        )
        pick = (pair_state[:, None] == states[None, :]).astype(jnp.float32)
        factor_re = jnp.dot(
            jnp.dot(pick, matrix[0], precision=HIGHEST), pick.T, precision=HIGHEST
        )
        factor_im = jnp.dot(
            jnp.dot(pick, matrix[1], precision=HIGHEST), pick.T, precision=HIGHEST
        )
        if real_part is None:
            real_part, imag_part = factor_re, factor_im
        else:
            real_part, imag_part = (
                real_part * factor_re - imag_part * factor_im,
                real_part * factor_im + imag_part * factor_re,
            )
    return (real_part, imag_part)


def group_gates(values, local_bits, group_bits, matrix):
    length = values.shape[1]
    groups = 2**group_bits
    low = local_bits - 2 * group_bits
    shaped = values.reshape(2, groups, groups, 2**low)
    shaped = lax.all_to_all(shaped, "grp", split_axis=2, concat_axis=2, tiled=True)
    real_op, imag_op = pair_operator(matrix, group_bits)
    block = shaped.reshape(2, groups * groups, 2**low)
    real_part = jnp.dot(
        real_op, block[0], precision=HIGHEST, preferred_element_type=jnp.float32
    ) - jnp.dot(imag_op, block[1], precision=HIGHEST, preferred_element_type=jnp.float32)
    imag_part = jnp.dot(
        real_op, block[1], precision=HIGHEST, preferred_element_type=jnp.float32
    ) + jnp.dot(imag_op, block[0], precision=HIGHEST, preferred_element_type=jnp.float32)
    shaped = jnp.stack([real_part, imag_part]).reshape(2, groups, groups, 2**low)
    shaped = lax.all_to_all(shaped, "grp", split_axis=2, concat_axis=2, tiled=True)
    return shaped.reshape(2, length)


def per_device(
    amplitudes, joined_gates, pair_gate, layout_in, layout_out, gate_qubits, spare_values
):
    length = amplitudes.shape[-1]
    local_bits = length.bit_length() - 1
    devices = lax.axis_size("dev")
    device_bits = devices.bit_length() - 1
    groups = lax.axis_size("grp")
    group_bits = groups.bit_length() - 1
    span_size = joined_gates.shape[-1]
    values = amplitudes.reshape(2, length)
    nothing = jnp.zeros((0,), jnp.int32)
    layout = layout_in[:local_bits]
    for gate_num in range(2):
        layout, source = arrange(layout, gate_qubits[gate_num], nothing)
        values = complex_gate(
            reorder(values, source).reshape(2, -1, span_size), joined_gates[gate_num]
        ).reshape(2, length)
    leaving = layout_out[local_bits : local_bits + device_bits]
    layout, source = arrange(layout, nothing, leaving)
    values = reorder(values, source)
    shaped = values.reshape(2, devices, length // devices)
    values = lax.all_to_all(shaped, "dev", split_axis=1, concat_axis=1, tiled=True).reshape(
        2, length
    )
    layout = jnp.concatenate(
        [layout[: local_bits - device_bits], layout_in[local_bits : local_bits + device_bits]]
    )
    for gate_num in range(2, 4):
        layout, source = arrange(layout, gate_qubits[gate_num], nothing)
        values = complex_gate(
            reorder(values, source).reshape(2, -1, span_size), joined_gates[gate_num]
        ).reshape(2, length)
    values = reorder(values, position_of(layout, layout_out[:local_bits]))
    values = values * spare_sign(length, spare_values)
    for bit_num in reversed(range(group_bits)):
        values = pair_exchange(values, local_bits - 1 - bit_num, bit_num, pair_gate)
    return values.reshape(amplitudes.shape)


def solution(mesh):
    in_specs = (P(None, "grp", "dev", None), P(), P(), P(), P(), P(), P())
    out_specs = P(None, "grp", "dev", None)
    return jax.shard_map(
        per_device, mesh=mesh, in_specs=in_specs, out_specs=out_specs, check_vma=False
    )
```

```python
import jax
import jax.numpy as jnp
from jax import lax
from jax.sharding import PartitionSpec as P

HIGHEST = lax.Precision.HIGHEST


def swapped(value, axis, bit):
    mask = 2**bit
    pairs = [(source, source ^ mask) for source in range(lax.axis_size(axis))]
    return lax.ppermute(value, axis, pairs)


def bit_table(bit_count):
    place = jnp.arange(2**bit_count, dtype=jnp.int32)[:, None]
    return jnp.right_shift(place, jnp.arange(bit_count, dtype=jnp.int32)[None, :]) & 1


def source_index(bit_order, bit_count):
    lane_bits = min(7, bit_count)
    lane_part = jnp.sum(
        jnp.left_shift(bit_table(lane_bits), bit_order[None, :lane_bits]), axis=1
    )
    row_part = jnp.sum(
        jnp.left_shift(bit_table(bit_count - lane_bits), bit_order[None, lane_bits:]), axis=1
    )
    return (row_part[:, None] + lane_part[None, :]).reshape(2**bit_count)


def reorder(values, source):
    bit_count = source.shape[0]
    length = 2**bit_count
    lane_bits = 7
    lanes = 2**lane_bits
    rows = length // lanes
    picked = source_index(source, bit_count)
    one_hot = (
        lax.broadcasted_iota(jnp.int32, (lanes, length), 0) == (picked & lanes - 1)[None, :]
    ).astype(jnp.float32)
    spread = jnp.dot(
        values.reshape(2 * rows, lanes),
        one_hot,
        precision=HIGHEST,
        preferred_element_type=jnp.float32,
    ).reshape(2, rows, length)
    row_hit = lax.broadcasted_iota(jnp.int32, (rows, length), 0) == jnp.right_shift(
        picked, lane_bits
    )[None, :]
    return jnp.sum(jnp.where(row_hit[None], spread, 0.0), axis=1)


def complex_gate(values, matrix):
    real_part = jnp.dot(
        values[0], matrix[0].T, precision=HIGHEST, preferred_element_type=jnp.float32
    ) - jnp.dot(values[1], matrix[1].T, precision=HIGHEST, preferred_element_type=jnp.float32)
    imag_part = jnp.dot(
        values[0], matrix[1].T, precision=HIGHEST, preferred_element_type=jnp.float32
    ) + jnp.dot(values[1], matrix[0].T, precision=HIGHEST, preferred_element_type=jnp.float32)
    return jnp.stack([real_part, imag_part])


def pair_apply(values, pos_a, pos_c, matrix):
    count_all = values.shape[1]
    lower_pos = min(pos_a, pos_c)
    upper_pos = max(pos_a, pos_c)
    shaped = values.reshape(
        2, count_all >> upper_pos + 1, 2, 1 << upper_pos - lower_pos - 1, 2, 1 << lower_pos
    )
    tensor = matrix.reshape(2, 2, 2, 2, 2)
    pattern = "uvwx,hwmxl->humvl"
    real_part = jnp.einsum(pattern, tensor[0], shaped[0], precision=HIGHEST) - jnp.einsum(
        pattern, tensor[1], shaped[1], precision=HIGHEST
    )
    imag_part = jnp.einsum(pattern, tensor[1], shaped[0], precision=HIGHEST) + jnp.einsum(
        pattern, tensor[0], shaped[1], precision=HIGHEST
    )
    return jnp.stack([real_part, imag_part]).reshape(2, count_all)


def spare_sign(count_all, spare_values):
    lane_bits = 7
    spare_count = spare_values.shape[0]
    row_bits = spare_count - lane_bits
    lane_parity = jnp.sum(bit_table(lane_bits) * spare_values[None, :lane_bits], axis=1)
    row_parity = jnp.sum(bit_table(row_bits) * spare_values[None, lane_bits:], axis=1)
    repeat = count_all // (2**spare_count)
    parity = row_parity[:, None] + lane_parity[None, :]
    sign = (1 - 2 * (parity & 1)).astype(jnp.float32).reshape(1, 2**spare_count)
    return jnp.broadcast_to(sign, (repeat, 2**spare_count)).reshape(count_all)


def position_of(layout, wanted):
    places = jnp.arange(layout.shape[0], dtype=jnp.int32)
    return jnp.sum(jnp.where(layout[None, :] == wanted[:, None], places[None, :], 0), axis=1)


def arrange(layout, leading, trailing):
    layout_len = layout.shape[0]
    lead_count = leading.shape[0]
    trail_count = trailing.shape[0]
    in_lead = layout[:, None] == leading[None, :]
    in_trail = layout[:, None] == trailing[None, :]
    lead_any = jnp.any(in_lead, axis=1)
    trail_any = jnp.any(in_trail, axis=1)
    remaining = jnp.logical_not(jnp.logical_or(lead_any, trail_any)).astype(jnp.int32)
    lead_rank = jnp.sum(in_lead * jnp.arange(lead_count, dtype=jnp.int32)[None, :], axis=1)
    trail_rank = (
        layout_len
        - trail_count
        + jnp.sum(in_trail * jnp.arange(trail_count, dtype=jnp.int32)[None, :], axis=1)
    )
    target = jnp.where(
        lead_any,
        lead_rank,
        jnp.where(trail_any, trail_rank, lead_count + jnp.cumsum(remaining) - 1),
    )
    places = jnp.arange(layout_len, dtype=jnp.int32)
    lands = target[None, :] == places[:, None]
    source = jnp.sum(jnp.where(lands, places[None, :], 0), axis=1)
    new_layout = jnp.sum(jnp.where(lands, layout[None, :], 0), axis=1)
    return (new_layout, source)


def halves(values, place_bit):
    count_all = values.shape[1]
    shaped = values.reshape(2, count_all >> place_bit + 1, 2, 1 << place_bit)
    return (shaped[:, :, 0], shaped[:, :, 1])


def rejoin(lower_half, upper_half, received, own_bit):
    keep_lower = own_bit == 0
    new_lower = jnp.where(keep_lower, lower_half, received)
    new_upper = jnp.where(keep_lower, received, upper_half)
    return jnp.stack([new_lower, new_upper], axis=2).reshape(2, -1)


def trade_group(values, place_bit, bit_num):
    lower_half, upper_half = halves(values, place_bit)
    own_bit = jnp.right_shift(lax.axis_index("grp"), bit_num) & 1
    outgoing = jnp.where(own_bit == 0, upper_half, lower_half)
    received = swapped(outgoing, "grp", bit_num)
    return rejoin(lower_half, upper_half, received, own_bit)


def pair_exchange(values, place_bit, bit_num, matrix):
    length = values.shape[1]
    lane_bits = 7
    rows = length >> lane_bits
    row_bit = place_bit - lane_bits
    own_bit = jnp.right_shift(lax.axis_index("grp"), bit_num) & 1
    received = swapped(values, "grp", bit_num)
    place = jnp.arange(rows, dtype=jnp.int32)
    mask = 1 << row_bit
    agree = (place[:, None] | mask) == (place[None, :] | mask)
    pair_bit = jnp.right_shift(place, row_bit) & 1
    states = jnp.arange(4, dtype=jnp.int32)
    pick_out = ((own_bit + 2 * pair_bit)[:, None] == states[None, :]).astype(jnp.float32)
    pick_par = ((1 - own_bit + 2 * pair_bit)[:, None] == states[None, :]).astype(jnp.float32)
    blocks = []
    for pick_in in (pick_out, pick_par):
        for part in range(2):
            coef = jnp.dot(
                jnp.dot(pick_out, matrix[part], precision=HIGHEST), pick_in.T, precision=HIGHEST
            )
            blocks.append(jnp.where(agree, coef, 0.0))
    own_re, own_im, par_re, par_im = blocks
    operator = jnp.concatenate(
        [
            jnp.concatenate([own_re, -own_im, par_re, -par_im], axis=1),
            jnp.concatenate([own_im, own_re, par_im, par_re], axis=1),
        ],
        axis=0,
    )
    stacked = jnp.concatenate(
        [values.reshape(2 * rows, -1), received.reshape(2 * rows, -1)], axis=0
    )
    out = jnp.dot(operator, stacked, precision=HIGHEST, preferred_element_type=jnp.float32)
    return out.reshape(2, length)


def pair_operator(matrix, group_bits):
    size = 2 ** (2 * group_bits)
    place = jnp.arange(size, dtype=jnp.int32)
    states = jnp.arange(4, dtype=jnp.int32)
    real_part = None
    imag_part = None
    for bit_num in range(group_bits):
        pair_state = (jnp.right_shift(place, bit_num) & 1) + 2 * (
            jnp.right_shift(place, 2 * group_bits - 1 - bit_num) & 1
        )
        pick = (pair_state[:, None] == states[None, :]).astype(jnp.float32)
        factor_re = jnp.dot(
            jnp.dot(pick, matrix[0], precision=HIGHEST), pick.T, precision=HIGHEST
        )
        factor_im = jnp.dot(
            jnp.dot(pick, matrix[1], precision=HIGHEST), pick.T, precision=HIGHEST
        )
        if real_part is None:
            real_part, imag_part = factor_re, factor_im
        else:
            real_part, imag_part = (
                real_part * factor_re - imag_part * factor_im,
                real_part * factor_im + imag_part * factor_re,
            )
    return (real_part, imag_part)


def group_gates(values, local_bits, group_bits, matrix):
    length = values.shape[1]
    groups = 2**group_bits
    low = local_bits - 2 * group_bits
    shaped = values.reshape(2, groups, groups, 2**low)
    shaped = lax.all_to_all(shaped, "grp", split_axis=2, concat_axis=2, tiled=True)
    real_op, imag_op = pair_operator(matrix, group_bits)
    block = shaped.reshape(2, groups * groups, 2**low)
    real_part = jnp.dot(
        real_op, block[0], precision=HIGHEST, preferred_element_type=jnp.float32
    ) - jnp.dot(imag_op, block[1], precision=HIGHEST, preferred_element_type=jnp.float32)
    imag_part = jnp.dot(
        real_op, block[1], precision=HIGHEST, preferred_element_type=jnp.float32
    ) + jnp.dot(imag_op, block[0], precision=HIGHEST, preferred_element_type=jnp.float32)
    shaped = jnp.stack([real_part, imag_part]).reshape(2, groups, groups, 2**low)
    shaped = lax.all_to_all(shaped, "grp", split_axis=2, concat_axis=2, tiled=True)
    return shaped.reshape(2, length)


def per_device(
    amplitudes, joined_gates, pair_gate, layout_in, layout_out, gate_qubits, spare_values
):
    length = amplitudes.shape[-1]
    local_bits = length.bit_length() - 1
    devices = lax.axis_size("dev")
    device_bits = devices.bit_length() - 1
    groups = lax.axis_size("grp")
    group_bits = groups.bit_length() - 1
    span_size = joined_gates.shape[-1]
    values = amplitudes.reshape(2, length)
    nothing = jnp.zeros((0,), jnp.int32)
    layout = layout_in[:local_bits]
    for gate_num in range(2):
        layout, source = arrange(layout, gate_qubits[gate_num], nothing)
        values = complex_gate(
            reorder(values, source).reshape(2, -1, span_size), joined_gates[gate_num]
        ).reshape(2, length)
    leaving = layout_out[local_bits : local_bits + device_bits]
    layout, source = arrange(layout, nothing, leaving)
    values = reorder(values, source)
    shaped = values.reshape(2, devices, length // devices)
    values = lax.all_to_all(shaped, "dev", split_axis=1, concat_axis=1, tiled=True).reshape(
        2, length
    )
    layout = jnp.concatenate(
        [layout[: local_bits - device_bits], layout_in[local_bits : local_bits + device_bits]]
    )
    for gate_num in range(2, 4):
        layout, source = arrange(layout, gate_qubits[gate_num], nothing)
        values = complex_gate(
            reorder(values, source).reshape(2, -1, span_size), joined_gates[gate_num]
        ).reshape(2, length)
    values = reorder(values, position_of(layout, layout_out[:local_bits]))
    values = values * spare_sign(length, spare_values)
    for bit_num in (3, 2, 0, 1)[:group_bits]:
        values = pair_exchange(values, local_bits - 1 - bit_num, bit_num, pair_gate)
    return values.reshape(amplitudes.shape)


def solution(mesh):
    in_specs = (P(None, "grp", "dev", None), P(), P(), P(), P(), P(), P())
    out_specs = P(None, "grp", "dev", None)
    return jax.shard_map(
        per_device, mesh=mesh, in_specs=in_specs, out_specs=out_specs, check_vma=False
    )
```
